512 devices in a mesh: seq: 32 (over y, x, core), tp: 16 (over z).
Axes of the slice: x: 4, y: 4, z: 16, core: 2. Of those that a mesh axis runs over, the one named last changes fastest.
Arguments:
- query_vectors: bfloat16 [24576, 4096], P('seq', 'tp'), may hold values from -6 to 6
- key_vectors: bfloat16 [24576, 4096], P('seq', 'tp'), may hold values from -6 to 6
- value_vectors: bfloat16 [24576, 4096], P('seq', 'tp'), may hold values from -6 to 6
- decay_exp: int32 [32, 24576], P('tp', 'seq'), may hold values from 0 to 16
- norm_gain: float32 [4096], P('tp'), may hold values from 0.25 to 1.75
- out_weight: bfloat16 [4096, 5120], P(None, 'tp'), may hold values from -0.09375 to 0.09375
- residual: bfloat16 [24576, 5120], P('seq', 'tp'), may hold values from -6 to 6
Outputs:
- layer_out: bfloat16 [24576, 5120], P('seq', 'tp')
The draws below stay inside these ranges and needn't reach their ends.
All inputs are finite; a program needn't handle non-finite values.
Results may differ from the reference program's by a relative error of at most 0.0051.
Values may be sent and summed in bfloat16 or wider, within the bound.
No kernel may reach another device: no remote copies, remote signals or barrier semaphores. Data moves between devices by JAX's collectives and lax.ppermute only.
A program may use at most 64 MiB of HBM per device.

```python
import jax
import jax.numpy as jnp
from jax import lax

D = 5120
HEAD_TOTAL = 32
HD = 128
TOK_DEV = 768
TOKEN_TOTAL = 24576


def widen(table):
    return jnp.repeat(table, TOK_DEV, axis=1)


def draw_decay_exp(key, part):
    lanes = jax.random.split(jax.random.fold_in(key, 7), 11)
    block_count = TOKEN_TOTAL // TOK_DEV
    grid = (HEAD_TOTAL, block_count)
    mixed_count = jax.random.randint(lanes[0], (), HEAD_TOTAL // 4, 3 * HEAD_TOTAL // 4 + 1)
    ranking = jax.random.permutation(lanes[1], HEAD_TOTAL)
    is_mixed = (ranking < mixed_count)[:, None]
    fast_block = widen(jax.random.randint(lanes[2], grid, 0, 2))
    spiky_decay_block = widen(jax.random.randint(lanes[3], grid, 0, 2))
    speed = widen(jax.random.randint(lanes[4], grid, 1, 3))
    repeat_interval = widen(jax.random.randint(lanes[5], grid, TOK_DEV // 6, TOK_DEV // 3 + 1))
    start_shift = widen(jax.random.randint(lanes[6], grid, 0, TOK_DEV // 6))
    place = jnp.arange(TOKEN_TOTAL, dtype=jnp.int32)
    inner_loop_body = (place % TOK_DEV)[None, :]
    gentle_exponent = jax.random.randint(lanes[7], (HEAD_TOTAL, TOKEN_TOTAL), speed, 2 * speed + 1)
    spike_exponent = jnp.where(jnp.remainder(inner_loop_body - start_shift, repeat_interval) == 0, 16, 0)
    quick_exponent = jnp.where(spiky_decay_block == 1, spike_exponent, gentle_exponent)
    coin = jax.random.randint(lanes[8], (HEAD_TOTAL, TOKEN_TOTAL), 0, 4 * TOK_DEV)
    quiet_exp = (coin < 3).astype(jnp.int32)
    spike_position = jax.random.randint(lanes[9], (HEAD_TOTAL, 2), 0, TOKEN_TOTAL)
    second_spike = jax.random.randint(lanes[10], (HEAD_TOTAL,), 5, 9)
    spike_length = jnp.stack([jnp.full((HEAD_TOTAL,), 16, jnp.int32), second_spike], axis=1)
    match_found = place[None, None, :] == spike_position[:, :, None]
    spike_group = jnp.max(jnp.where(match_found, spike_length[:, :, None], 0), axis=1)
    quiet_exp = jnp.maximum(quiet_exp, spike_group)
    use_fast = jnp.logical_and(is_mixed, fast_block == 1)
    return jnp.where(use_fast, quick_exponent, quiet_exp).astype(jnp.int32)


def levels(own_key, shape, cuts, low, high):
    level, own = 1.0, jax.random.fold_in(own_key, 6)
    for axis_at, shards_of in cuts:
        steps = jnp.exp(jax.random.uniform(jax.random.fold_in(own, axis_at), (shards_of,), jnp.float32, low / len(cuts), high / len(cuts)))
        level = level * jnp.repeat(steps, shape[axis_at] // shards_of).reshape([-1 if axis == axis_at else 1 for axis in range(len(shape))])
    return level


def noise(stream_key, dims, deviation, bound, cuts=(), kind=jnp.bfloat16):
    result = deviation * jax.random.normal(stream_key, dims, jnp.float32)
    if cuts:
        result = result * levels(stream_key, dims, cuts, -0.22, 0.18)
    return jnp.clip(result, -bound, bound).astype(kind)


def setup_inputs(seed: int = 0) -> dict:
    splits = jax.random.split(jax.random.key(seed), 8)
    query_vectors = noise(splits[0], (TOKEN_TOTAL, HEAD_TOTAL * HD), 1.0, 6.0, ((0, 32), (1, 16)))
    key_vectors = noise(splits[1], (TOKEN_TOTAL, HEAD_TOTAL * HD), 1.0, 6.0, ((0, 32), (1, 16)))
    value_vectors = noise(splits[2], (TOKEN_TOTAL, HEAD_TOTAL * HD), 1.0, 6.0, ((0, 32), (1, 16)))
    decay_exp = draw_decay_exp(jax.random.fold_in(splits[7], 71), 0)
    norm_gain = jnp.clip(1.0 + 0.15 * jax.random.normal(splits[4], (HEAD_TOTAL * HD,), jnp.float32), 0.25, 1.75)
    out_weight = noise(splits[5], (HEAD_TOTAL * HD, D), (HEAD_TOTAL * HD) ** -0.5, 0.09375, ((1, 16),))
    residual = noise(splits[6], (TOKEN_TOTAL, D), 1.0, 6.0, ((0, 32), (1, 16)))
    return dict(query_vectors=query_vectors, key_vectors=key_vectors, value_vectors=value_vectors, decay_exp=decay_exp, norm_gain=norm_gain, out_weight=out_weight, residual=residual)


def factor(exponents):
    return jnp.exp2(-exponents.astype(jnp.float32) / 16.0)

def one_head(inputs):
    query_head, key_head, value_head, exp_head, gain_head = inputs
    block_count = TOKEN_TOTAL // TOK_DEV
    query_blocks = query_head.reshape(block_count, TOK_DEV, HD).astype(jnp.float32)
    key_blocks = key_head.reshape(block_count, TOK_DEV, HD).astype(jnp.float32)
    value_blocks = value_head.reshape(block_count, TOK_DEV, HD).astype(jnp.float32)
    local_exp = jnp.cumsum(exp_head.reshape(block_count, TOK_DEV), axis=1).astype(jnp.int32)
    block_exp = local_exp[:, -1]
    scores = jnp.einsum('btd,bsd->bts', query_blocks, key_blocks)
    exp_gap = jnp.abs(local_exp[:, :, None] - local_exp[:, None, :])
    local_weights = (scores * factor(exp_gap)).astype(jnp.bfloat16)
    local_part = jnp.einsum('bts,bsd->btd', local_weights.astype(jnp.float32), value_blocks)
    keys_fwd = (key_blocks * factor(block_exp[:, None] - local_exp)[:, :, None]).astype(jnp.bfloat16)
    keys_bwd = (key_blocks * factor(local_exp)[:, :, None]).astype(jnp.bfloat16)
    summary_fwd = jnp.einsum('bsd,bse->bde', keys_fwd.astype(jnp.float32), value_blocks)
    summary_bwd = jnp.einsum('bsd,bse->bde', keys_bwd.astype(jnp.float32), value_blocks)
    block_decay = factor(block_exp)

    def advance(running, pair):
        decay, summary = pair
        return (decay * running + summary, running)
    zero_state = jnp.zeros((HD, HD), jnp.float32)
    _, state_fwd = lax.scan(advance, zero_state, (block_decay, summary_fwd))
    _, state_bwd = lax.scan(advance, zero_state, (block_decay, summary_bwd), reverse=True)
    state_fwd = state_fwd.astype(jnp.bfloat16).astype(jnp.float32)
    state_bwd = state_bwd.astype(jnp.bfloat16).astype(jnp.float32)
    remote_fwd = jnp.einsum('btd,bde->bte', query_blocks, state_fwd) * factor(local_exp)[:, :, None]
    remote_bwd = jnp.einsum('btd,bde->bte', query_blocks, state_bwd) * factor(block_exp[:, None] - local_exp)[:, :, None]
    attention = (local_part + remote_fwd + remote_bwd).reshape(TOKEN_TOTAL, HD)
    scale = lax.rsqrt(lax.optimization_barrier(jnp.mean(attention * attention, axis=-1, keepdims=True)) + 1e-06)
    return (attention * scale * gain_head[None, :]).astype(jnp.bfloat16)

def reference(query_vectors, key_vectors, value_vectors, decay_exp, norm_gain, out_weight, residual):
    query_heads = query_vectors.reshape(TOKEN_TOTAL, HEAD_TOTAL, HD).transpose(1, 0, 2)
    key_heads = key_vectors.reshape(TOKEN_TOTAL, HEAD_TOTAL, HD).transpose(1, 0, 2)
    value_heads = value_vectors.reshape(TOKEN_TOTAL, HEAD_TOTAL, HD).transpose(1, 0, 2)
    gain_heads = norm_gain.reshape(HEAD_TOTAL, HD)
    normed = lax.map(one_head, (query_heads, key_heads, value_heads, decay_exp, gain_heads))
    normed = normed.transpose(1, 0, 2).reshape(TOKEN_TOTAL, HEAD_TOTAL * HD)
    mixed = jnp.dot(normed, out_weight, preferred_element_type=jnp.float32)
    return (residual.astype(jnp.float32) + mixed).astype(jnp.bfloat16)
```

```python
import jax
import jax.numpy as jnp
from jax import lax
from jax.sharding import PartitionSpec as P

HD = 128


def factor(exponents):
    return jnp.exp2(-exponents.astype(jnp.float32) / 16.0)


def prefix_scan(decay, summary, direction):
    seq_count = lax.axis_size("seq")
    inc_p, inc_s = decay, summary
    exc_p = jnp.ones_like(decay)
    exc_s = jnp.zeros_like(summary)
    shift = 1
    while shift < seq_count:
        if direction > 0:
            pairs = [(i, i + shift) for i in range(seq_count - shift)]
        else:
            pairs = [(i + shift, i) for i in range(seq_count - shift)]
        packed = jnp.concatenate(
            [inc_s, jnp.broadcast_to(inc_p[:, None, None], (inc_p.shape[0], 8, HD))], axis=1
        )
        packed = lax.ppermute(packed, "seq", pairs)
        got_s, got_p = packed[:, :HD], packed[:, HD, 0]
        exc_s = exc_p[:, None, None] * got_s + exc_s
        exc_p = got_p * exc_p
        if 2 * shift < seq_count:
            inc_s = inc_p[:, None, None] * got_s + inc_s
            inc_p = got_p * inc_p
        shift *= 2
    return exc_s


def local(query_vectors, key_vectors, value_vectors, decay_exp, norm_gain, out_weight, residual):
    tok_rows = query_vectors.shape[0]
    head_count = decay_exp.shape[0]
    query_heads = query_vectors.reshape(tok_rows, head_count, HD)
    key_heads = key_vectors.reshape(tok_rows, head_count, HD)
    value_heads = value_vectors.reshape(tok_rows, head_count, HD)
    local_exp = jnp.cumsum(decay_exp, axis=1)
    block_exp = local_exp[:, -1]
    local_rows = local_exp.T
    scores = jnp.einsum("thd,shd->hts", query_heads, key_heads, preferred_element_type=jnp.float32)
    exp_gap = jnp.abs(local_exp[:, :, None] - local_exp[:, None, :])
    local_weights = (scores * factor(exp_gap)).astype(jnp.bfloat16)
    local_part = jnp.einsum(
        "hts,shd->thd", local_weights, value_heads, preferred_element_type=jnp.float32
    )
    tail_factor = factor(block_exp[None, :] - local_rows)
    head_factor = factor(local_rows)
    keys_fwd = (key_heads * tail_factor[:, :, None]).astype(jnp.bfloat16)
    keys_bwd = (key_heads * head_factor[:, :, None]).astype(jnp.bfloat16)
    summary_fwd = jnp.einsum(
        "shd,she->hde", keys_fwd, value_heads, preferred_element_type=jnp.float32
    )
    summary_bwd = jnp.einsum(
        "shd,she->hde", keys_bwd, value_heads, preferred_element_type=jnp.float32
    )
    block_decay = factor(block_exp)
    state_fwd = prefix_scan(block_decay, summary_fwd, 1)
    state_bwd = prefix_scan(block_decay, summary_bwd, -1)
    state_fwd = state_fwd.astype(jnp.bfloat16)
    state_bwd = state_bwd.astype(jnp.bfloat16)
    remote_fwd = (
        jnp.einsum("thd,hde->the", query_heads, state_fwd, preferred_element_type=jnp.float32)
        * head_factor[:, :, None]
    )
    remote_bwd = (
        jnp.einsum("thd,hde->the", query_heads, state_bwd, preferred_element_type=jnp.float32)
        * tail_factor[:, :, None]
    )
    attention = local_part + remote_fwd + remote_bwd
    scale = lax.rsqrt(jnp.mean(attention * attention, axis=-1, keepdims=True) + 1e-06)
    normed = (attention * scale * norm_gain.reshape(head_count, HD)[None, :, :]).astype(
        jnp.bfloat16
    )
    normed = normed.reshape(tok_rows, head_count * HD)
    mixed = jnp.dot(
        lax.all_gather(normed, "tp", axis=1, tiled=True),
        out_weight,
        preferred_element_type=jnp.float32,
    )
    return (residual.astype(jnp.float32) + mixed).astype(jnp.bfloat16)


def solution(mesh):
    in_specs = (
        P("seq", "tp"),
        P("seq", "tp"),
        P("seq", "tp"),
        P("tp", "seq"),
        P("tp"),
        P(None, "tp"),
        P("seq", "tp"),
    )
    out_specs = P("seq", "tp")
    return jax.shard_map(local, mesh=mesh, in_specs=in_specs, out_specs=out_specs, check_vma=False)
```

```python
import jax
import jax.numpy as jnp
from jax import lax
from jax.sharding import PartitionSpec as P

HD = 128


def factor(exponents):
    return jnp.exp2(-exponents.astype(jnp.float32) / 16.0)


def block_scan(decay, summary_fwd, summary_bwd):
    seq_count = lax.axis_size("seq")
    me = lax.axis_index("seq")
    heads = decay.shape[0]
    total_p, total_f, total_b = decay, summary_fwd, summary_bwd
    prefix_pf = jnp.ones_like(decay)
    prefix_pb = jnp.ones_like(decay)
    prefix_f = jnp.zeros_like(summary_fwd)
    prefix_b = jnp.zeros_like(summary_bwd)
    shift = 1
    while shift < seq_count:
        pairs = [(i, i ^ shift) for i in range(seq_count)]
        packed = jnp.concatenate(
            [total_f, total_b, jnp.broadcast_to(total_p[:, None, None], (heads, 8, HD))], axis=1
        )
        packed = lax.ppermute(packed, "seq", pairs)
        got_f, got_b, got_p = packed[:, :HD], packed[:, HD : 2 * HD], packed[:, 2 * HD, 0]
        lower = (me & shift) != 0
        prefix_f = prefix_f + jnp.where(lower, prefix_pf, 0.0)[:, None, None] * got_f
        prefix_b = prefix_b + jnp.where(lower, 0.0, prefix_pb)[:, None, None] * got_b
        prefix_pf = jnp.where(lower, got_p * prefix_pf, prefix_pf)
        prefix_pb = jnp.where(lower, prefix_pb, got_p * prefix_pb)
        if 2 * shift < seq_count:
            own_f = jnp.where(lower, 1.0, got_p)[:, None, None]
            new_f = jnp.where(lower, total_p, 1.0)[:, None, None]
            own_b = jnp.where(lower, got_p, 1.0)[:, None, None]
            new_b = jnp.where(lower, 1.0, total_p)[:, None, None]
            total_f = own_f * total_f + new_f * got_f
            total_b = own_b * total_b + new_b * got_b
            total_p = total_p * got_p
        shift *= 2
    return prefix_f, prefix_b


def local(query_vectors, key_vectors, value_vectors, decay_exp, norm_gain, out_weight, residual):
    tok_rows = query_vectors.shape[0]
    head_count = decay_exp.shape[0]
    query_heads = query_vectors.reshape(tok_rows, head_count, HD)
    key_heads = key_vectors.reshape(tok_rows, head_count, HD)
    value_heads = value_vectors.reshape(tok_rows, head_count, HD)
    local_exp = jnp.cumsum(decay_exp, axis=1)
    block_exp = local_exp[:, -1]
    local_rows = local_exp.T
    scores = jnp.einsum("thd,shd->hts", query_heads, key_heads, preferred_element_type=jnp.float32)
    exp_gap = jnp.abs(local_exp[:, :, None] - local_exp[:, None, :])
    local_weights = (scores * factor(exp_gap)).astype(jnp.bfloat16)
    local_part = jnp.einsum(
        "hts,shd->thd", local_weights, value_heads, preferred_element_type=jnp.float32
    )
    tail_factor = factor(block_exp[None, :] - local_rows)
    head_factor = factor(local_rows)
    keys_fwd = (key_heads * tail_factor[:, :, None]).astype(jnp.bfloat16)
    keys_bwd = (key_heads * head_factor[:, :, None]).astype(jnp.bfloat16)
    summary_fwd = jnp.einsum(
        "shd,she->hde", keys_fwd, value_heads, preferred_element_type=jnp.float32
    )
    summary_bwd = jnp.einsum(
        "shd,she->hde", keys_bwd, value_heads, preferred_element_type=jnp.float32
    )
    block_decay = factor(block_exp)
    state_fwd, state_bwd = block_scan(block_decay, summary_fwd, summary_bwd)
    state_fwd = state_fwd.astype(jnp.bfloat16)
    state_bwd = state_bwd.astype(jnp.bfloat16)
    remote_fwd = (
        jnp.einsum("thd,hde->the", query_heads, state_fwd, preferred_element_type=jnp.float32)
        * head_factor[:, :, None]
    )
    remote_bwd = (
        jnp.einsum("thd,hde->the", query_heads, state_bwd, preferred_element_type=jnp.float32)
        * tail_factor[:, :, None]
    )
    attention = local_part + remote_fwd + remote_bwd
    scale = lax.rsqrt(jnp.mean(attention * attention, axis=-1, keepdims=True) + 1e-06)
    normed = (attention * scale * norm_gain.reshape(head_count, HD)[None, :, :]).astype(
        jnp.bfloat16
    )
    normed = normed.reshape(tok_rows, head_count * HD)
    mixed = jnp.dot(
        lax.all_gather(normed, "tp", axis=1, tiled=True),
        out_weight,
        preferred_element_type=jnp.float32,
    )
    return (residual.astype(jnp.float32) + mixed).astype(jnp.bfloat16)


def solution(mesh):
    in_specs = (
        P("seq", "tp"),
        P("seq", "tp"),
        P("seq", "tp"),
        P("tp", "seq"),
        P("tp"),
        P(None, "tp"),
        P("seq", "tp"),
    )
    out_specs = P("seq", "tp")
    return jax.shard_map(local, mesh=mesh, in_specs=in_specs, out_specs=out_specs, check_vma=False)
```

```python
import jax
import jax.numpy as jnp
from jax import lax
from jax.sharding import PartitionSpec as P

HD = 128


def factor(exponents):
    return jnp.exp2(-exponents.astype(jnp.float32) / 16.0)


def pack(summary, decay):
    heads = decay.shape[0]
    return jnp.concatenate(
        [summary, jnp.broadcast_to(decay[:, None, None], (heads, 8, HD))], axis=1
    )


def block_scan(decay, summary_fwd, summary_bwd):
    seq_count = lax.axis_size("seq")
    me = lax.axis_index("seq")
    second = (me % 2) == 1
    chip = me // 2
    mine = jnp.where(second, summary_bwd, summary_fwd)
    other = jnp.where(second, summary_fwd, summary_bwd)
    got = lax.ppermute(pack(other, decay), "seq", [(i, i ^ 1) for i in range(seq_count)])
    got_s, got_p = got[:, :HD], got[:, HD, 0]
    total_s = got_p[:, None, None] * mine + got_s
    total_p = decay * got_p
    prefix_s = jnp.zeros_like(mine)
    prefix_p = jnp.ones_like(decay)
    shift = 1
    while 2 * shift < seq_count:
        pairs = [(i, i ^ (2 * shift)) for i in range(seq_count)]
        got = lax.ppermute(pack(total_s, total_p), "seq", pairs)
        got_s, got_p = got[:, :HD], got[:, HD, 0]
        earlier = ((chip & shift) != 0) != second
        prefix_s = prefix_s + jnp.where(earlier, prefix_p, 0.0)[:, None, None] * got_s
        prefix_p = jnp.where(earlier, got_p * prefix_p, prefix_p)
        if 4 * shift < seq_count:
            own = jnp.where(earlier, 1.0, got_p)[:, None, None]
            new = jnp.where(earlier, total_p, 1.0)[:, None, None]
            total_s = own * total_s + new * got_s
            total_p = total_p * got_p
        shift *= 2
    handed = lax.ppermute(
        decay[:, None, None] * prefix_s + mine, "seq", [(i, i ^ 1) for i in range(seq_count)]
    )
    state_fwd = jnp.where(second, handed, prefix_s)
    state_bwd = jnp.where(second, prefix_s, handed)
    return state_fwd, state_bwd


def local(query_vectors, key_vectors, value_vectors, decay_exp, norm_gain, out_weight, residual):
    tok_rows = query_vectors.shape[0]
    head_count = decay_exp.shape[0]
    query_heads = query_vectors.reshape(tok_rows, head_count, HD)
    key_heads = key_vectors.reshape(tok_rows, head_count, HD)
    value_heads = value_vectors.reshape(tok_rows, head_count, HD)
    local_exp = jnp.cumsum(decay_exp, axis=1)
    block_exp = local_exp[:, -1]
    local_rows = local_exp.T
    scores = jnp.einsum("thd,shd->hts", query_heads, key_heads, preferred_element_type=jnp.float32)
    exp_gap = jnp.abs(local_exp[:, :, None] - local_exp[:, None, :])
    local_weights = (scores * factor(exp_gap)).astype(jnp.bfloat16)
    local_part = jnp.einsum(
        "hts,shd->thd", local_weights, value_heads, preferred_element_type=jnp.float32
    )
    tail_factor = factor(block_exp[None, :] - local_rows)
    head_factor = factor(local_rows)
    keys_fwd = (key_heads * tail_factor[:, :, None]).astype(jnp.bfloat16)
    keys_bwd = (key_heads * head_factor[:, :, None]).astype(jnp.bfloat16)
    summary_fwd = jnp.einsum(
        "shd,she->hde", keys_fwd, value_heads, preferred_element_type=jnp.float32
    )
    summary_bwd = jnp.einsum(
        "shd,she->hde", keys_bwd, value_heads, preferred_element_type=jnp.float32
    )
    block_decay = factor(block_exp)
    state_fwd, state_bwd = block_scan(block_decay, summary_fwd, summary_bwd)
    state_fwd = state_fwd.astype(jnp.bfloat16)
    state_bwd = state_bwd.astype(jnp.bfloat16)
    remote_fwd = (
        jnp.einsum("thd,hde->the", query_heads, state_fwd, preferred_element_type=jnp.float32)
        * head_factor[:, :, None]
    )
    remote_bwd = (
        jnp.einsum("thd,hde->the", query_heads, state_bwd, preferred_element_type=jnp.float32)
        * tail_factor[:, :, None]
    )
    attention = local_part + remote_fwd + remote_bwd
    scale = lax.rsqrt(jnp.mean(attention * attention, axis=-1, keepdims=True) + 1e-06)
    normed = (attention * scale * norm_gain.reshape(head_count, HD)[None, :, :]).astype(
        jnp.bfloat16
    )
    normed = normed.reshape(tok_rows, head_count * HD)
    mixed = jnp.dot(
        lax.all_gather(normed, "tp", axis=1, tiled=True),
        out_weight,
        preferred_element_type=jnp.float32,
    )
    return (residual.astype(jnp.float32) + mixed).astype(jnp.bfloat16)


def solution(mesh):
    in_specs = (
        P("seq", "tp"),
        P("seq", "tp"),
        P("seq", "tp"),
        P("tp", "seq"),
        P("tp"),
        P(None, "tp"),
        P("seq", "tp"),
    )
    out_specs = P("seq", "tp")
    return jax.shard_map(local, mesh=mesh, in_specs=in_specs, out_specs=out_specs, check_vma=False)
```

```python
import jax
import jax.numpy as jnp
from jax import lax
from jax.sharding import PartitionSpec as P

HD = 128


def factor(exponents):
    return jnp.exp2(-exponents.astype(jnp.float32) / 16.0)


def pack(summary, decay):
    heads = decay.shape[0]
    return jnp.concatenate(
        [summary, jnp.broadcast_to(decay[:, None, None], (heads, 8, HD))], axis=1
    )


def unpack(packed):
    return packed[:, :HD], packed[:, HD, 0]


def gather_line(total_s, total_p, line, stride, seq_count):
    got = []
    for shift in range(1, line):
        pairs = []
        for i in range(seq_count):
            at = (i // stride) % line
            step = -shift if i % 2 else shift
            pairs.append((i, i + (((at + step) % line) - at) * stride))
        got.append(unpack(lax.ppermute(pack(total_s, total_p), "seq", pairs)))
    return got


def block_scan(decay, summary_fwd, summary_bwd):
    seq_count = lax.axis_size("seq")
    line = 4
    me = lax.axis_index("seq")
    second = (me % 2) == 1
    x = (me // 2) % line
    y = me // (2 * line)
    pos_x = jnp.where(second, line - 1 - x, x)
    pos_y = jnp.where(second, line - 1 - y, y)
    mine = jnp.where(second, summary_bwd, summary_fwd)
    other = jnp.where(second, summary_fwd, summary_bwd)
    got_s, got_p = unpack(
        lax.ppermute(pack(other, decay), "seq", [(i, i ^ 1) for i in range(seq_count)])
    )
    chip_s = got_p[:, None, None] * mine + got_s
    chip_p = decay * got_p

    def prefix(got, pos):
        acc_s = jnp.zeros_like(chip_s)
        acc_p = jnp.ones_like(chip_p)
        for m, (s, p) in enumerate(got, start=1):
            valid = pos >= m
            acc_s = acc_s + jnp.where(valid, acc_p, 0.0)[:, None, None] * s
            acc_p = jnp.where(valid, acc_p * p, acc_p)
        return acc_s, acc_p

    row = gather_line(chip_s, chip_p, line, 2, seq_count)
    row_prefix_s, row_prefix_p = prefix(row, pos_x)
    row_s = chip_p[:, None, None] * row_prefix_s + chip_s
    row_p = chip_p
    for m in range(1, line):
        s, p = row[line - 1 - m]
        valid = pos_x <= line - 1 - m
        row_s = jnp.where(valid, p, 1.0)[:, None, None] * row_s + jnp.where(valid, 1.0, 0.0) * s
        row_p = row_p * p
    col = gather_line(row_s, row_p, line, 2 * line, seq_count)
    col_prefix_s, _ = prefix(col, pos_y)
    state = row_prefix_p[:, None, None] * col_prefix_s + row_prefix_s
    handed = lax.ppermute(
        decay[:, None, None] * state + mine, "seq", [(i, i ^ 1) for i in range(seq_count)]
    )
    state_fwd = jnp.where(second, handed, state)
    state_bwd = jnp.where(second, state, handed)
    return state_fwd, state_bwd


def local(query_vectors, key_vectors, value_vectors, decay_exp, norm_gain, out_weight, residual):
    tok_rows = query_vectors.shape[0]
    head_count = decay_exp.shape[0]
    query_heads = query_vectors.reshape(tok_rows, head_count, HD)
    key_heads = key_vectors.reshape(tok_rows, head_count, HD)
    value_heads = value_vectors.reshape(tok_rows, head_count, HD)
    local_exp = jnp.cumsum(decay_exp, axis=1)
    block_exp = local_exp[:, -1]
    local_rows = local_exp.T
    scores = jnp.einsum("thd,shd->hts", query_heads, key_heads, preferred_element_type=jnp.float32)
    exp_gap = jnp.abs(local_exp[:, :, None] - local_exp[:, None, :])
    local_weights = (scores * factor(exp_gap)).astype(jnp.bfloat16)
    local_part = jnp.einsum(
        "hts,shd->thd", local_weights, value_heads, preferred_element_type=jnp.float32
    )
    tail_factor = factor(block_exp[None, :] - local_rows)
    head_factor = factor(local_rows)
    keys_fwd = (key_heads * tail_factor[:, :, None]).astype(jnp.bfloat16)
    keys_bwd = (key_heads * head_factor[:, :, None]).astype(jnp.bfloat16)
    summary_fwd = jnp.einsum(
        "shd,she->hde", keys_fwd, value_heads, preferred_element_type=jnp.float32
    )
    summary_bwd = jnp.einsum(
        "shd,she->hde", keys_bwd, value_heads, preferred_element_type=jnp.float32
    )
    block_decay = factor(block_exp)
    state_fwd, state_bwd = block_scan(block_decay, summary_fwd, summary_bwd)
    state_fwd = state_fwd.astype(jnp.bfloat16)
    state_bwd = state_bwd.astype(jnp.bfloat16)
    remote_fwd = (
        jnp.einsum("thd,hde->the", query_heads, state_fwd, preferred_element_type=jnp.float32)
        * head_factor[:, :, None]
    )
    remote_bwd = (
        jnp.einsum("thd,hde->the", query_heads, state_bwd, preferred_element_type=jnp.float32)
        * tail_factor[:, :, None]
    )
    attention = local_part + remote_fwd + remote_bwd
    scale = lax.rsqrt(jnp.mean(attention * attention, axis=-1, keepdims=True) + 1e-06)
    normed = (attention * scale * norm_gain.reshape(head_count, HD)[None, :, :]).astype(
        jnp.bfloat16
    )
    normed = normed.reshape(tok_rows, head_count * HD)
    mixed = jnp.dot(
        lax.all_gather(normed, "tp", axis=1, tiled=True),
        out_weight,
        preferred_element_type=jnp.float32,
    )
    return (residual.astype(jnp.float32) + mixed).astype(jnp.bfloat16)


def solution(mesh):
    in_specs = (
        P("seq", "tp"),
        P("seq", "tp"),
        P("seq", "tp"),
        P("tp", "seq"),
        P("tp"),
        P(None, "tp"),
        P("seq", "tp"),
    )
    out_specs = P("seq", "tp")
    return jax.shard_map(local, mesh=mesh, in_specs=in_specs, out_specs=out_specs, check_vma=False)
```

```python
import jax
import jax.numpy as jnp
from jax import lax
from jax.sharding import PartitionSpec as P

HD = 128


def factor(exponents):
    return jnp.exp2(-exponents.astype(jnp.float32) / 16.0)


def pack(summary, decay):
    heads = decay.shape[0]
    return jnp.concatenate(
        [summary, jnp.broadcast_to(decay[:, None, None], (heads, 8, HD))], axis=1
    )


def unpack(packed):
    return packed[:, :HD], packed[:, HD, 0]


def gather_line(total_s, total_p, line, stride, seq_count):
    got = []
    for shift in range(1, line):
        pairs = []
        for i in range(seq_count):
            at = (i // stride) % line
            step = -shift if i % 2 else shift
            pairs.append((i, i + (((at + step) % line) - at) * stride))
        got.append(unpack(lax.ppermute(pack(total_s, total_p), "seq", pairs)))
    return got


def block_scan(decay, summary_fwd, summary_bwd):
    seq_count = lax.axis_size("seq")
    line = 4
    me = lax.axis_index("seq")
    second = (me % 2) == 1
    x = (me // 2) % line
    y = me // (2 * line)
    pos_x = jnp.where(second, line - 1 - x, x)
    pos_y = jnp.where(second, line - 1 - y, y)
    mine = jnp.where(second, summary_bwd, summary_fwd)
    other = jnp.where(second, summary_fwd, summary_bwd)
    got_s, got_p = unpack(
        lax.ppermute(pack(other, decay), "seq", [(i, i ^ 1) for i in range(seq_count)])
    )
    chip_s = got_p[:, None, None] * mine + got_s
    chip_p = decay * got_p

    def prefix(got, pos):
        acc_s = jnp.zeros_like(chip_s)
        acc_p = jnp.ones_like(chip_p)
        for m, (s, p) in enumerate(got, start=1):
            valid = pos >= m
            acc_s = acc_s + jnp.where(valid, acc_p, 0.0)[:, None, None] * s
            acc_p = jnp.where(valid, acc_p * p, acc_p)
        return acc_s, acc_p

    row = gather_line(chip_s, chip_p, line, 2, seq_count)
    row_prefix_s, row_prefix_p = prefix(row, pos_x)
    row_s = chip_p[:, None, None] * row_prefix_s + chip_s
    row_p = chip_p
    for m in range(1, line):
        s, p = row[line - 1 - m]
        valid = pos_x <= line - 1 - m
        row_s = jnp.where(valid, p, 1.0)[:, None, None] * row_s + jnp.where(valid, 1.0, 0.0) * s
        row_p = row_p * p
    col = gather_line(row_s, row_p, line, 2 * line, seq_count)
    col_prefix_s, _ = prefix(col, pos_y)
    state = row_prefix_p[:, None, None] * col_prefix_s + row_prefix_s
    handed = lax.ppermute(
        decay[:, None, None] * state + mine, "seq", [(i, i ^ 1) for i in range(seq_count)]
    )
    state_fwd = jnp.where(second, handed, state)
    state_bwd = jnp.where(second, state, handed)
    return state_fwd, state_bwd


def ring_project(normed, out_weight):
    tp_count = lax.axis_size("tp")
    me = lax.axis_index("tp")
    width = normed.shape[1]

    def part(shard, source):
        rows = lax.dynamic_slice_in_dim(out_weight, source * width, width, axis=0)
        return jnp.dot(shard, rows, preferred_element_type=jnp.float32)

    up = [(j, (j + 1) % tp_count) for j in range(tp_count)]
    down = [(j, (j - 1) % tp_count) for j in range(tp_count)]
    mixed = part(normed, me)
    rising, falling = normed, normed
    for step in range(1, tp_count // 2 + 1):
        rising = lax.ppermute(rising, "tp", up)
        if step < tp_count - step:
            falling = lax.ppermute(falling, "tp", down)
        mixed = mixed + part(rising, (me - step) % tp_count)
        if step < tp_count - step:
            mixed = mixed + part(falling, (me + step) % tp_count)
    return mixed


def local(query_vectors, key_vectors, value_vectors, decay_exp, norm_gain, out_weight, residual):
    tok_rows = query_vectors.shape[0]
    head_count = decay_exp.shape[0]
    query_heads = query_vectors.reshape(tok_rows, head_count, HD)
    key_heads = key_vectors.reshape(tok_rows, head_count, HD)
    value_heads = value_vectors.reshape(tok_rows, head_count, HD)
    local_exp = jnp.cumsum(decay_exp, axis=1)
    block_exp = local_exp[:, -1]
    local_rows = local_exp.T
    scores = jnp.einsum("thd,shd->hts", query_heads, key_heads, preferred_element_type=jnp.float32)
    exp_gap = jnp.abs(local_exp[:, :, None] - local_exp[:, None, :])
    local_weights = (scores * factor(exp_gap)).astype(jnp.bfloat16)
    local_part = jnp.einsum(
        "hts,shd->thd", local_weights, value_heads, preferred_element_type=jnp.float32
    )
    tail_factor = factor(block_exp[None, :] - local_rows)
    head_factor = factor(local_rows)
    keys_fwd = (key_heads * tail_factor[:, :, None]).astype(jnp.bfloat16)
    keys_bwd = (key_heads * head_factor[:, :, None]).astype(jnp.bfloat16)
    summary_fwd = jnp.einsum(
        "shd,she->hde", keys_fwd, value_heads, preferred_element_type=jnp.float32
    )
    summary_bwd = jnp.einsum(
        "shd,she->hde", keys_bwd, value_heads, preferred_element_type=jnp.float32
    )
    block_decay = factor(block_exp)
    state_fwd, state_bwd = block_scan(block_decay, summary_fwd, summary_bwd)
    state_fwd = state_fwd.astype(jnp.bfloat16)
    state_bwd = state_bwd.astype(jnp.bfloat16)
    remote_fwd = (
        jnp.einsum("thd,hde->the", query_heads, state_fwd, preferred_element_type=jnp.float32)
        * head_factor[:, :, None]
    )
    remote_bwd = (
        jnp.einsum("thd,hde->the", query_heads, state_bwd, preferred_element_type=jnp.float32)
        * tail_factor[:, :, None]
    )
    attention = local_part + remote_fwd + remote_bwd
    scale = lax.rsqrt(jnp.mean(attention * attention, axis=-1, keepdims=True) + 1e-06)
    normed = (attention * scale * norm_gain.reshape(head_count, HD)[None, :, :]).astype(
        jnp.bfloat16
    )
    normed = normed.reshape(tok_rows, head_count * HD)
    mixed = ring_project(normed, out_weight)
    return (residual.astype(jnp.float32) + mixed).astype(jnp.bfloat16)


def solution(mesh):
    in_specs = (
        P("seq", "tp"),
        P("seq", "tp"),
        P("seq", "tp"),
        P("tp", "seq"),
        P("tp"),
        P(None, "tp"),
        P("seq", "tp"),
    )
    out_specs = P("seq", "tp")
    return jax.shard_map(local, mesh=mesh, in_specs=in_specs, out_specs=out_specs, check_vma=False)
```

```python
import jax
import jax.numpy as jnp
from jax import lax
from jax.sharding import PartitionSpec as P

HD = 128


def factor(exponents):
    return jnp.exp2(-exponents.astype(jnp.float32) / 16.0)


def pack(summary, decay):
    heads = decay.shape[0]
    return jnp.concatenate(
        [summary, jnp.broadcast_to(decay[:, None, None], (heads, 8, HD))], axis=1
    )


def unpack(packed):
    return packed[:, :HD], packed[:, HD, 0]


def gather_line(total_s, total_p, line, stride, seq_count):
    got = []
    for shift in range(1, line):
        pairs = []
        for i in range(seq_count):
            at = (i // stride) % line
            step = -shift if i % 2 else shift
            pairs.append((i, i + (((at + step) % line) - at) * stride))
        got.append(unpack(lax.ppermute(pack(total_s, total_p), "seq", pairs)))
    return got


def block_scan(decay, summary_fwd, summary_bwd):
    seq_count = lax.axis_size("seq")
    line = 4
    me = lax.axis_index("seq")
    second = (me % 2) == 1
    x = (me // 2) % line
    y = me // (2 * line)
    pos_x = jnp.where(second, line - 1 - x, x)
    pos_y = jnp.where(second, line - 1 - y, y)
    mine = jnp.where(second, summary_bwd, summary_fwd)
    other = jnp.where(second, summary_fwd, summary_bwd)
    got_s, got_p = unpack(
        lax.ppermute(pack(other, decay), "seq", [(i, i ^ 1) for i in range(seq_count)])
    )
    chip_s = got_p[:, None, None] * mine + got_s
    chip_p = decay * got_p

    def prefix(got, pos):
        acc_s = jnp.zeros_like(chip_s)
        acc_p = jnp.ones_like(chip_p)
        for m, (s, p) in enumerate(got, start=1):
            valid = pos >= m
            acc_s = acc_s + jnp.where(valid, acc_p, 0.0)[:, None, None] * s
            acc_p = jnp.where(valid, acc_p * p, acc_p)
        return acc_s, acc_p

    row = gather_line(chip_s, chip_p, line, 2, seq_count)
    row_prefix_s, row_prefix_p = prefix(row, pos_x)
    row_s = chip_p[:, None, None] * row_prefix_s + chip_s
    row_p = chip_p
    for m in range(1, line):
        s, p = row[line - 1 - m]
        valid = pos_x <= line - 1 - m
        row_s = jnp.where(valid, p, 1.0)[:, None, None] * row_s + jnp.where(valid, 1.0, 0.0) * s
        row_p = row_p * p
    col = gather_line(row_s, row_p, line, 2 * line, seq_count)
    col_prefix_s, _ = prefix(col, pos_y)
    state = row_prefix_p[:, None, None] * col_prefix_s + row_prefix_s
    handed = lax.ppermute(
        decay[:, None, None] * state + mine, "seq", [(i, i ^ 1) for i in range(seq_count)]
    )
    state_fwd = jnp.where(second, handed, state)
    state_bwd = jnp.where(second, state, handed)
    return state_fwd, state_bwd


def ring_project(normed, out_weight):
    tp_count = lax.axis_size("tp")
    me = lax.axis_index("tp")
    width = normed.shape[1]
    half = width // 2
    gathered = lax.all_gather(normed[:, :half], "tp", axis=1, tiled=True)
    first_rows = out_weight.reshape(tp_count, width, -1)[:, :half].reshape(tp_count * half, -1)

    def part(shard, source):
        rows = lax.dynamic_slice_in_dim(out_weight, source * width + half, half, axis=0)
        return jnp.dot(shard, rows, preferred_element_type=jnp.float32)

    up = [(j, (j + 1) % tp_count) for j in range(tp_count)]
    down = [(j, (j - 1) % tp_count) for j in range(tp_count)]
    own = normed[:, half:]
    mixed = part(own, me)
    rising, falling = own, own
    for step in range(1, tp_count // 2 + 1):
        rising = lax.ppermute(rising, "tp", up)
        if step < tp_count - step:
            falling = lax.ppermute(falling, "tp", down)
        mixed = mixed + part(rising, (me - step) % tp_count)
        if step < tp_count - step:
            mixed = mixed + part(falling, (me + step) % tp_count)
    return mixed + jnp.dot(gathered, first_rows, preferred_element_type=jnp.float32)


def local(query_vectors, key_vectors, value_vectors, decay_exp, norm_gain, out_weight, residual):
    tok_rows = query_vectors.shape[0]
    head_count = decay_exp.shape[0]
    query_heads = query_vectors.reshape(tok_rows, head_count, HD)
    key_heads = key_vectors.reshape(tok_rows, head_count, HD)
    value_heads = value_vectors.reshape(tok_rows, head_count, HD)
    local_exp = jnp.cumsum(decay_exp, axis=1)
    block_exp = local_exp[:, -1]
    local_rows = local_exp.T
    scores = jnp.einsum("thd,shd->hts", query_heads, key_heads, preferred_element_type=jnp.float32)
    exp_gap = jnp.abs(local_exp[:, :, None] - local_exp[:, None, :])
    local_weights = (scores * factor(exp_gap)).astype(jnp.bfloat16)
    local_part = jnp.einsum(
        "hts,shd->thd", local_weights, value_heads, preferred_element_type=jnp.float32
    )
    tail_factor = factor(block_exp[None, :] - local_rows)
    head_factor = factor(local_rows)
    keys_fwd = (key_heads * tail_factor[:, :, None]).astype(jnp.bfloat16)
    keys_bwd = (key_heads * head_factor[:, :, None]).astype(jnp.bfloat16)
    summary_fwd = jnp.einsum(
        "shd,she->hde", keys_fwd, value_heads, preferred_element_type=jnp.float32
    )
    summary_bwd = jnp.einsum(
        "shd,she->hde", keys_bwd, value_heads, preferred_element_type=jnp.float32
    )
    block_decay = factor(block_exp)
    state_fwd, state_bwd = block_scan(block_decay, summary_fwd, summary_bwd)
    state_fwd = state_fwd.astype(jnp.bfloat16)
    state_bwd = state_bwd.astype(jnp.bfloat16)
    remote_fwd = (
        jnp.einsum("thd,hde->the", query_heads, state_fwd, preferred_element_type=jnp.float32)
        * head_factor[:, :, None]
    )
    remote_bwd = (
        jnp.einsum("thd,hde->the", query_heads, state_bwd, preferred_element_type=jnp.float32)
        * tail_factor[:, :, None]
    )
    attention = local_part + remote_fwd + remote_bwd
    scale = lax.rsqrt(jnp.mean(attention * attention, axis=-1, keepdims=True) + 1e-06)
    normed = (attention * scale * norm_gain.reshape(head_count, HD)[None, :, :]).astype(
        jnp.bfloat16
    )
    normed = normed.reshape(tok_rows, head_count * HD)
    mixed = ring_project(normed, out_weight)
    return (residual.astype(jnp.float32) + mixed).astype(jnp.bfloat16)


def solution(mesh):
    in_specs = (
        P("seq", "tp"),
        P("seq", "tp"),
        P("seq", "tp"),
        P("tp", "seq"),
        P("tp"),
        P(None, "tp"),
        P("seq", "tp"),
    )
    out_specs = P("seq", "tp")
    return jax.shard_map(local, mesh=mesh, in_specs=in_specs, out_specs=out_specs, check_vma=False)
```

```python
import jax
import jax.numpy as jnp
from jax import lax
from jax.sharding import PartitionSpec as P

HD = 128


def factor(exponents):
    return jnp.exp2(-exponents.astype(jnp.float32) / 16.0)


def pack(summary, decay):
    heads = decay.shape[0]
    return jnp.concatenate(
        [summary, jnp.broadcast_to(decay[:, None, None], (heads, 8, HD))], axis=1
    )


def unpack(packed):
    return packed[:, :HD], packed[:, HD, 0]


def gather_line(total_s, total_p, line, stride, seq_count):
    got = []
    for shift in range(1, line):
        pairs = []
        for i in range(seq_count):
            at = (i // stride) % line
            step = -shift if i % 2 else shift
            pairs.append((i, i + (((at + step) % line) - at) * stride))
        got.append(unpack(lax.ppermute(pack(total_s, total_p), "seq", pairs)))
    return got


def block_scan(decay, summary_fwd, summary_bwd):
    seq_count = lax.axis_size("seq")
    line = 4
    me = lax.axis_index("seq")
    second = (me % 2) == 1
    x = (me // 2) % line
    y = me // (2 * line)
    pos_x = jnp.where(second, line - 1 - x, x)
    pos_y = jnp.where(second, line - 1 - y, y)
    mine = jnp.where(second, summary_bwd, summary_fwd)
    other = jnp.where(second, summary_fwd, summary_bwd)
    got_s, got_p = unpack(
        lax.ppermute(pack(other, decay), "seq", [(i, i ^ 1) for i in range(seq_count)])
    )
    chip_s = got_p[:, None, None] * mine + got_s
    chip_p = decay * got_p

    def prefix(got, pos):
        acc_s = jnp.zeros_like(chip_s)
        acc_p = jnp.ones_like(chip_p)
        for m, (s, p) in enumerate(got, start=1):
            valid = pos >= m
            acc_s = acc_s + jnp.where(valid, acc_p, 0.0)[:, None, None] * s
            acc_p = jnp.where(valid, acc_p * p, acc_p)
        return acc_s, acc_p

    row = gather_line(chip_s, chip_p, line, 2, seq_count)
    row_prefix_s, row_prefix_p = prefix(row, pos_x)
    row_s = chip_p[:, None, None] * row_prefix_s + chip_s
    row_p = chip_p
    for m in range(1, line):
        s, p = row[line - 1 - m]
        valid = pos_x <= line - 1 - m
        row_s = jnp.where(valid, p, 1.0)[:, None, None] * row_s + jnp.where(valid, 1.0, 0.0) * s
        row_p = row_p * p
    col = gather_line(row_s, row_p, line, 2 * line, seq_count)
    col_prefix_s, _ = prefix(col, pos_y)
    state = row_prefix_p[:, None, None] * col_prefix_s + row_prefix_s
    handed = lax.ppermute(
        decay[:, None, None] * state + mine, "seq", [(i, i ^ 1) for i in range(seq_count)]
    )
    state_fwd = jnp.where(second, handed, state)
    state_bwd = jnp.where(second, state, handed)
    return state_fwd, state_bwd


def ring_project(normed, out_weight):
    tp_count = lax.axis_size("tp")
    me = lax.axis_index("tp")
    width = normed.shape[1]
    half = width // 2

    def part(shard, source, offset=0):
        rows = lax.dynamic_slice_in_dim(
            out_weight, source * width + offset, shard.shape[1], axis=0
        )
        return jnp.dot(shard, rows, preferred_element_type=jnp.float32)

    up = [(j, (j + 1) % tp_count) for j in range(tp_count)]
    down = [(j, (j - 1) % tp_count) for j in range(tp_count)]
    mixed = part(normed, me)
    rising, falling = normed, normed
    for step in range(1, tp_count // 2):
        rising = lax.ppermute(rising, "tp", up)
        falling = lax.ppermute(falling, "tp", down)
        mixed = mixed + part(rising, (me - step) % tp_count)
        mixed = mixed + part(falling, (me + step) % tp_count)
    far = (me + tp_count // 2) % tp_count
    rising = lax.ppermute(rising[:, :half], "tp", up)
    falling = lax.ppermute(falling[:, half:], "tp", down)
    mixed = mixed + part(rising, far)
    mixed = mixed + part(falling, far, half)
    return mixed


def local(query_vectors, key_vectors, value_vectors, decay_exp, norm_gain, out_weight, residual):
    tok_rows = query_vectors.shape[0]
    head_count = decay_exp.shape[0]
    query_heads = query_vectors.reshape(tok_rows, head_count, HD)
    key_heads = key_vectors.reshape(tok_rows, head_count, HD)
    value_heads = value_vectors.reshape(tok_rows, head_count, HD)
    local_exp = jnp.cumsum(decay_exp, axis=1)
    block_exp = local_exp[:, -1]
    local_rows = local_exp.T
    scores = jnp.einsum("thd,shd->hts", query_heads, key_heads, preferred_element_type=jnp.float32)
    exp_gap = jnp.abs(local_exp[:, :, None] - local_exp[:, None, :])
    local_weights = (scores * factor(exp_gap)).astype(jnp.bfloat16)
    local_part = jnp.einsum(
        "hts,shd->thd", local_weights, value_heads, preferred_element_type=jnp.float32
    )
    tail_factor = factor(block_exp[None, :] - local_rows)
    head_factor = factor(local_rows)
    keys_fwd = (key_heads * tail_factor[:, :, None]).astype(jnp.bfloat16)
    keys_bwd = (key_heads * head_factor[:, :, None]).astype(jnp.bfloat16)
    summary_fwd = jnp.einsum(
        "shd,she->hde", keys_fwd, value_heads, preferred_element_type=jnp.float32
    )
    summary_bwd = jnp.einsum(
        "shd,she->hde", keys_bwd, value_heads, preferred_element_type=jnp.float32
    )
    block_decay = factor(block_exp)
    state_fwd, state_bwd = block_scan(block_decay, summary_fwd, summary_bwd)
    state_fwd = state_fwd.astype(jnp.bfloat16)
    state_bwd = state_bwd.astype(jnp.bfloat16)
    remote_fwd = (
        jnp.einsum("thd,hde->the", query_heads, state_fwd, preferred_element_type=jnp.float32)
        * head_factor[:, :, None]
    )
    remote_bwd = (
        jnp.einsum("thd,hde->the", query_heads, state_bwd, preferred_element_type=jnp.float32)
        * tail_factor[:, :, None]
    )
    attention = local_part + remote_fwd + remote_bwd
    scale = lax.rsqrt(jnp.mean(attention * attention, axis=-1, keepdims=True) + 1e-06)
    normed = (attention * scale * norm_gain.reshape(head_count, HD)[None, :, :]).astype(
        jnp.bfloat16
    )
    normed = normed.reshape(tok_rows, head_count * HD)
    mixed = ring_project(normed, out_weight)
    return (residual.astype(jnp.float32) + mixed).astype(jnp.bfloat16)


def solution(mesh):
    in_specs = (
        P("seq", "tp"),
        P("seq", "tp"),
        P("seq", "tp"),
        P("tp", "seq"),
        P("tp"),
        P(None, "tp"),
        P("seq", "tp"),
    )
    out_specs = P("seq", "tp")
    return jax.shard_map(local, mesh=mesh, in_specs=in_specs, out_specs=out_specs, check_vma=False)
```

```python
import jax
import jax.numpy as jnp
from jax import lax
from jax.sharding import PartitionSpec as P

HD = 128


def factor(exponents):
    return jnp.exp2(-exponents.astype(jnp.float32) / 16.0)


def pack(summary, decay):
    heads = decay.shape[0]
    return jnp.concatenate(
        [summary, jnp.broadcast_to(decay[:, None, None], (heads, 8, HD))], axis=1
    )


def unpack(packed):
    return packed[:, :HD], packed[:, HD, 0]


def gather_line(total_s, total_p, line, stride, seq_count):
    got = []
    for shift in range(1, line):
        pairs = []
        for i in range(seq_count):
            at = (i // stride) % line
            step = -shift if i % 2 else shift
            pairs.append((i, i + (((at + step) % line) - at) * stride))
        got.append(unpack(lax.ppermute(pack(total_s, total_p), "seq", pairs)))
    return got


def block_scan(decay, summary_fwd, summary_bwd):
    seq_count = lax.axis_size("seq")
    line = 4
    me = lax.axis_index("seq")
    second = (me % 2) == 1
    x = (me // 2) % line
    y = me // (2 * line)
    pos_x = jnp.where(second, line - 1 - x, x)
    pos_y = jnp.where(second, line - 1 - y, y)
    mine = jnp.where(second, summary_bwd, summary_fwd)
    other = jnp.where(second, summary_fwd, summary_bwd)
    got_s, got_p = unpack(
        lax.ppermute(pack(other, decay), "seq", [(i, i ^ 1) for i in range(seq_count)])
    )
    chip_s = got_p[:, None, None] * mine + got_s
    chip_p = decay * got_p

    def prefix(got, pos):
        acc_s = jnp.zeros_like(chip_s)
        acc_p = jnp.ones_like(chip_p)
        for m, (s, p) in enumerate(got, start=1):
            valid = pos >= m
            acc_s = acc_s + jnp.where(valid, acc_p, 0.0)[:, None, None] * s
            acc_p = jnp.where(valid, acc_p * p, acc_p)
        return acc_s, acc_p

    row = gather_line(chip_s, chip_p, line, 2, seq_count)
    row_prefix_s, row_prefix_p = prefix(row, pos_x)
    row_s = chip_p[:, None, None] * row_prefix_s + chip_s
    row_p = chip_p
    for m in range(1, line):
        s, p = row[line - 1 - m]
        valid = pos_x <= line - 1 - m
        row_s = jnp.where(valid, p, 1.0)[:, None, None] * row_s + jnp.where(valid, 1.0, 0.0) * s
        row_p = row_p * p
    col = gather_line(row_s, row_p, line, 2 * line, seq_count)
    col_prefix_s, _ = prefix(col, pos_y)
    state = row_prefix_p[:, None, None] * col_prefix_s + row_prefix_s
    handed = lax.ppermute(
        decay[:, None, None] * state + mine, "seq", [(i, i ^ 1) for i in range(seq_count)]
    )
    state_fwd = jnp.where(second, handed, state)
    state_bwd = jnp.where(second, state, handed)
    return state_fwd, state_bwd


def local(query_vectors, key_vectors, value_vectors, decay_exp, norm_gain, out_weight, residual):
    tok_rows = query_vectors.shape[0]
    head_count = decay_exp.shape[0]
    query_heads = query_vectors.reshape(tok_rows, head_count, HD)
    key_heads = key_vectors.reshape(tok_rows, head_count, HD)
    value_heads = value_vectors.reshape(tok_rows, head_count, HD)
    local_exp = jnp.cumsum(decay_exp, axis=1)
    block_exp = local_exp[:, -1]
    local_rows = local_exp.T
    scores = jnp.einsum("thd,shd->hts", query_heads, key_heads, preferred_element_type=jnp.float32)
    exp_gap = jnp.abs(local_exp[:, :, None] - local_exp[:, None, :])
    local_weights = (scores * factor(exp_gap)).astype(jnp.bfloat16)
    local_part = jnp.einsum(
        "hts,shd->thd", local_weights, value_heads, preferred_element_type=jnp.float32
    )
    tail_factor = factor(block_exp[None, :] - local_rows)
    head_factor = factor(local_rows)
    keys_fwd = (key_heads * tail_factor[:, :, None]).astype(jnp.bfloat16)
    keys_bwd = (key_heads * head_factor[:, :, None]).astype(jnp.bfloat16)
    summary_fwd = jnp.einsum(
        "shd,she->hde", keys_fwd, value_heads, preferred_element_type=jnp.float32
    )
    summary_bwd = jnp.einsum(
        "shd,she->hde", keys_bwd, value_heads, preferred_element_type=jnp.float32
    )
    block_decay = factor(block_exp)
    state_fwd, state_bwd = block_scan(block_decay, summary_fwd, summary_bwd)
    state_fwd = state_fwd.astype(jnp.bfloat16)
    state_bwd = state_bwd.astype(jnp.bfloat16)
    remote_fwd = (
        jnp.einsum("thd,hde->the", query_heads, state_fwd, preferred_element_type=jnp.float32)
        * head_factor[:, :, None]
    )
    remote_bwd = (
        jnp.einsum("thd,hde->the", query_heads, state_bwd, preferred_element_type=jnp.float32)
        * tail_factor[:, :, None]
    )
    attention = local_part + remote_fwd + remote_bwd
    scale = lax.rsqrt(jnp.mean(attention * attention, axis=-1, keepdims=True) + 1e-06)
    normed = (attention * scale * norm_gain.reshape(head_count, HD)[None, :, :]).astype(
        jnp.bfloat16
    )
    normed = normed.reshape(tok_rows, head_count * HD)
    tp_count = lax.axis_size("tp")
    rows = out_weight.reshape(tp_count, head_count, HD, -1)
    mixed = None
    for head in range(head_count):
        gathered = lax.all_gather(normed[:, head * HD : (head + 1) * HD], "tp", axis=1, tiled=True)
        part = jnp.dot(
            gathered, rows[:, head].reshape(tp_count * HD, -1), preferred_element_type=jnp.float32
        )
        mixed = part if mixed is None else mixed + part
    return (residual.astype(jnp.float32) + mixed).astype(jnp.bfloat16)


def solution(mesh):
    in_specs = (
        P("seq", "tp"),
        P("seq", "tp"),
        P("seq", "tp"),
        P("tp", "seq"),
        P("tp"),
        P(None, "tp"),
        P("seq", "tp"),
    )
    out_specs = P("seq", "tp")
    return jax.shard_map(local, mesh=mesh, in_specs=in_specs, out_specs=out_specs, check_vma=False)
```

```python
import jax
import jax.numpy as jnp
from jax import lax
from jax.sharding import PartitionSpec as P

HD = 128


def factor(exponents):
    return jnp.exp2(-exponents.astype(jnp.float32) / 16.0)


def pack(summary, decay):
    heads = decay.shape[0]
    return jnp.concatenate(
        [summary, jnp.broadcast_to(decay[:, None, None], (heads, 8, HD))], axis=1
    )


def unpack(packed):
    return packed[:, :HD], packed[:, HD, 0]


def gather_line(total_s, total_p, line, stride, seq_count):
    got = []
    for shift in range(1, line):
        pairs = []
        for i in range(seq_count):
            at = (i // stride) % line
            step = -shift if i % 2 else shift
            pairs.append((i, i + (((at + step) % line) - at) * stride))
        got.append(unpack(lax.ppermute(pack(total_s, total_p), "seq", pairs)))
    return got


def block_scan(decay, mine, other):
    seq_count = lax.axis_size("seq")
    line = 4
    me = lax.axis_index("seq")
    second = (me % 2) == 1
    x = (me // 2) % line
    y = me // (2 * line)
    pos_x = jnp.where(second, line - 1 - x, x)
    pos_y = jnp.where(second, line - 1 - y, y)
    got_s, got_p = unpack(
        lax.ppermute(pack(other, decay), "seq", [(i, i ^ 1) for i in range(seq_count)])
    )
    chip_s = got_p[:, None, None] * mine + got_s
    chip_p = decay * got_p

    def prefix(got, pos):
        acc_s = jnp.zeros_like(chip_s)
        acc_p = jnp.ones_like(chip_p)
        for m, (s, p) in enumerate(got, start=1):
            valid = pos >= m
            acc_s = acc_s + jnp.where(valid, acc_p, 0.0)[:, None, None] * s
            acc_p = jnp.where(valid, acc_p * p, acc_p)
        return acc_s, acc_p

    row = gather_line(chip_s, chip_p, line, 2, seq_count)
    row_prefix_s, row_prefix_p = prefix(row, pos_x)
    row_s = chip_p[:, None, None] * row_prefix_s + chip_s
    row_p = chip_p
    for m in range(1, line):
        s, p = row[line - 1 - m]
        valid = pos_x <= line - 1 - m
        row_s = jnp.where(valid, p, 1.0)[:, None, None] * row_s + jnp.where(valid, 1.0, 0.0) * s
        row_p = row_p * p
    col = gather_line(row_s, row_p, line, 2 * line, seq_count)
    col_prefix_s, _ = prefix(col, pos_y)
    state = row_prefix_p[:, None, None] * col_prefix_s + row_prefix_s
    handed = lax.ppermute(
        decay[:, None, None] * state + mine, "seq", [(i, i ^ 1) for i in range(seq_count)]
    )
    state_fwd = jnp.where(second, handed, state)
    state_bwd = jnp.where(second, state, handed)
    return state_fwd, state_bwd


def local(query_vectors, key_vectors, value_vectors, decay_exp, norm_gain, out_weight, residual):
    tok_rows = query_vectors.shape[0]
    head_count = decay_exp.shape[0]
    query_heads = query_vectors.reshape(tok_rows, head_count, HD)
    key_heads = key_vectors.reshape(tok_rows, head_count, HD)
    value_heads = value_vectors.reshape(tok_rows, head_count, HD)
    local_exp = jnp.cumsum(decay_exp, axis=1)
    block_exp = local_exp[:, -1]
    local_rows = local_exp.T
    scores = jnp.einsum("thd,shd->hts", query_heads, key_heads, preferred_element_type=jnp.float32)
    exp_gap = jnp.abs(local_exp[:, :, None] - local_exp[:, None, :])
    local_weights = (scores * factor(exp_gap)).astype(jnp.bfloat16)
    local_part = jnp.einsum(
        "hts,shd->thd", local_weights, value_heads, preferred_element_type=jnp.float32
    )
    tail_factor = factor(block_exp[None, :] - local_rows)
    head_factor = factor(local_rows)
    second = (lax.axis_index("seq") % 2) == 1
    mine_factor = jnp.where(second, head_factor, tail_factor)
    other_factor = jnp.where(second, tail_factor, head_factor)
    keys_mine = (key_heads * mine_factor[:, :, None]).astype(jnp.bfloat16)
    keys_other = (key_heads * other_factor[:, :, None]).astype(jnp.bfloat16)
    summary_mine = jnp.einsum(
        "shd,she->hde", keys_mine, value_heads, preferred_element_type=jnp.float32
    )
    summary_other = jnp.einsum(
        "shd,she->hde", keys_other, value_heads, preferred_element_type=jnp.float32
    )
    block_decay = factor(block_exp)
    state_fwd, state_bwd = block_scan(block_decay, summary_mine, summary_other)
    state_fwd = state_fwd.astype(jnp.bfloat16)
    state_bwd = state_bwd.astype(jnp.bfloat16)
    remote_fwd = (
        jnp.einsum("thd,hde->the", query_heads, state_fwd, preferred_element_type=jnp.float32)
        * head_factor[:, :, None]
    )
    remote_bwd = (
        jnp.einsum("thd,hde->the", query_heads, state_bwd, preferred_element_type=jnp.float32)
        * tail_factor[:, :, None]
    )
    attention = local_part + remote_fwd + remote_bwd
    scale = lax.rsqrt(jnp.mean(attention * attention, axis=-1, keepdims=True) + 1e-06)
    normed = (attention * scale * norm_gain.reshape(head_count, HD)[None, :, :]).astype(
        jnp.bfloat16
    )
    normed = normed.reshape(tok_rows, head_count * HD)
    mixed = jnp.dot(
        lax.all_gather(normed, "tp", axis=1, tiled=True),
        out_weight,
        preferred_element_type=jnp.float32,
    )
    return (residual.astype(jnp.float32) + mixed).astype(jnp.bfloat16)


def solution(mesh):
    in_specs = (
        P("seq", "tp"),
        P("seq", "tp"),
        P("seq", "tp"),
        P("tp", "seq"),
        P("tp"),
        P(None, "tp"),
        P("seq", "tp"),
    )
    out_specs = P("seq", "tp")
    return jax.shard_map(local, mesh=mesh, in_specs=in_specs, out_specs=out_specs, check_vma=False)
```

```python
import jax
import jax.numpy as jnp
from jax import lax
from jax.sharding import PartitionSpec as P

HD = 128


def factor(exponents):
    return jnp.exp2(-exponents.astype(jnp.float32) / 16.0)


def pack(summary, decay):
    heads = decay.shape[0]
    return jnp.concatenate(
        [summary, jnp.broadcast_to(decay[:, None, None], (heads, 8, HD))], axis=1
    )


def gather_line(packed, line, stride, seq_count):
    got = []
    for shift in range(1, line):
        pairs = []
        for i in range(seq_count):
            at = (i // stride) % line
            step = -shift if i % 2 else shift
            pairs.append((i, i + (((at + step) % line) - at) * stride))
        got.append(lax.ppermute(packed, "seq", pairs))
    return got


def block_scan(decay, mine, other):
    seq_count = lax.axis_size("seq")
    line = 4
    me = lax.axis_index("seq")
    second = (me % 2) == 1
    x = (me // 2) % line
    y = me // (2 * line)
    pos_x = jnp.where(second, line - 1 - x, x)
    pos_y = jnp.where(second, line - 1 - y, y)
    is_s = lax.broadcasted_iota(jnp.int32, (1, HD + 8, 1), 1) < HD

    def decay_of(packed):
        return packed[:, HD : HD + 1, 0:1]

    own = pack(mine, decay)
    got = lax.ppermute(pack(other, decay), "seq", [(i, i ^ 1) for i in range(seq_count)])
    chip = decay_of(got) * own + jnp.where(is_s, got, 0.0)

    def prefix(got, pos):
        acc = jnp.where(is_s, 0.0, 1.0) * jnp.ones_like(chip)
        for m, part in enumerate(got, start=1):
            acc = jnp.where(pos >= m, decay_of(acc) * part + jnp.where(is_s, acc, 0.0), acc)
        return acc

    row = gather_line(chip, line, 2, seq_count)
    row_prefix = prefix(row, pos_x)
    total = jnp.where(is_s, decay_of(chip) * row_prefix + chip, chip)
    for m in range(1, line):
        part = row[line - 1 - m]
        valid = pos_x <= line - 1 - m
        total = jnp.where(
            is_s, jnp.where(valid, decay_of(part) * total + part, total), total * decay_of(part)
        )
    col = gather_line(total, line, 2 * line, seq_count)
    col_prefix = prefix(col, pos_y)
    state = (decay_of(row_prefix) * col_prefix + row_prefix)[:, :HD]
    handed = lax.ppermute(
        decay[:, None, None] * state + mine, "seq", [(i, i ^ 1) for i in range(seq_count)]
    )
    state_fwd = jnp.where(second, handed, state)
    state_bwd = jnp.where(second, state, handed)
    return state_fwd, state_bwd


def local(query_vectors, key_vectors, value_vectors, decay_exp, norm_gain, out_weight, residual):
    tok_rows = query_vectors.shape[0]
    head_count = decay_exp.shape[0]
    query_heads = query_vectors.reshape(tok_rows, head_count, HD)
    key_heads = key_vectors.reshape(tok_rows, head_count, HD)
    value_heads = value_vectors.reshape(tok_rows, head_count, HD)
    local_exp = jnp.cumsum(decay_exp, axis=1)
    block_exp = local_exp[:, -1]
    local_rows = local_exp.T
    scores = jnp.einsum("thd,shd->hts", query_heads, key_heads, preferred_element_type=jnp.float32)
    exp_gap = jnp.abs(local_exp[:, :, None] - local_exp[:, None, :])
    local_weights = (scores * factor(exp_gap)).astype(jnp.bfloat16)
    local_part = jnp.einsum(
        "hts,shd->thd", local_weights, value_heads, preferred_element_type=jnp.float32
    )
    tail_factor = factor(block_exp[None, :] - local_rows)
    head_factor = factor(local_rows)
    second = (lax.axis_index("seq") % 2) == 1
    mine_factor = jnp.where(second, head_factor, tail_factor)
    other_factor = jnp.where(second, tail_factor, head_factor)
    keys_mine = (key_heads * mine_factor[:, :, None]).astype(jnp.bfloat16)
    keys_other = (key_heads * other_factor[:, :, None]).astype(jnp.bfloat16)
    summary_mine = jnp.einsum(
        "shd,she->hde", keys_mine, value_heads, preferred_element_type=jnp.float32
    )
    summary_other = jnp.einsum(
        "shd,she->hde", keys_other, value_heads, preferred_element_type=jnp.float32
    )
    block_decay = factor(block_exp)
    state_fwd, state_bwd = block_scan(block_decay, summary_mine, summary_other)
    state_fwd = state_fwd.astype(jnp.bfloat16)
    state_bwd = state_bwd.astype(jnp.bfloat16)
    remote_fwd = (
        jnp.einsum("thd,hde->the", query_heads, state_fwd, preferred_element_type=jnp.float32)
        * head_factor[:, :, None]
    )
    remote_bwd = (
        jnp.einsum("thd,hde->the", query_heads, state_bwd, preferred_element_type=jnp.float32)
        * tail_factor[:, :, None]
    )
    attention = local_part + remote_fwd + remote_bwd
    scale = lax.rsqrt(jnp.mean(attention * attention, axis=-1, keepdims=True) + 1e-06)
    normed = (attention * scale * norm_gain.reshape(head_count, HD)[None, :, :]).astype(
        jnp.bfloat16
    )
    normed = normed.reshape(tok_rows, head_count * HD)
    mixed = jnp.dot(
        lax.all_gather(normed, "tp", axis=1, tiled=True),
        out_weight,
        preferred_element_type=jnp.float32,
    )
    return (residual.astype(jnp.float32) + mixed).astype(jnp.bfloat16)


def solution(mesh):
    in_specs = (
        P("seq", "tp"),
        P("seq", "tp"),
        P("seq", "tp"),
        P("tp", "seq"),
        P("tp"),
        P(None, "tp"),
        P("seq", "tp"),
    )
    out_specs = P("seq", "tp")
    return jax.shard_map(local, mesh=mesh, in_specs=in_specs, out_specs=out_specs, check_vma=False)
```

```python
import jax
import jax.numpy as jnp
from jax import lax
from jax.sharding import PartitionSpec as P

HD = 128


def factor(exponents):
    return jnp.exp2(-exponents.astype(jnp.float32) / 16.0)


def pack(summary, decay):
    heads = decay.shape[0]
    return jnp.concatenate(
        [summary, jnp.broadcast_to(decay[:, None, None], (heads, 8, HD))], axis=1
    )


def gather_line(packed, line, stride, seq_count):
    got = []
    for shift in range(1, line):
        pairs = []
        for i in range(seq_count):
            at = (i // stride) % line
            step = -shift if i % 2 else shift
            pairs.append((i, i + (((at + step) % line) - at) * stride))
        got.append(lax.ppermute(packed, "seq", pairs))
    return got


def block_scan(decay, mine, other, extra_fn, extra_args):
    seq_count = lax.axis_size("seq")
    line = 4
    me = lax.axis_index("seq")
    second = (me % 2) == 1
    x = (me // 2) % line
    y = me // (2 * line)
    pos_x = jnp.where(second, line - 1 - x, x)
    pos_y = jnp.where(second, line - 1 - y, y)
    is_s = lax.broadcasted_iota(jnp.int32, (1, HD + 8, 1), 1) < HD

    def decay_of(packed):
        return packed[:, HD : HD + 1, 0:1]

    own = pack(mine, decay)
    got = lax.ppermute(pack(other, decay), "seq", [(i, i ^ 1) for i in range(seq_count)])
    chip = decay_of(got) * own + jnp.where(is_s, got, 0.0)
    chip, extra_args = lax.optimization_barrier((chip, extra_args))
    extra = extra_fn(*extra_args)

    def prefix(got, pos):
        acc = jnp.where(is_s, 0.0, 1.0) * jnp.ones_like(chip)
        for m, part in enumerate(got, start=1):
            acc = jnp.where(pos >= m, decay_of(acc) * part + jnp.where(is_s, acc, 0.0), acc)
        return acc

    row = gather_line(chip, line, 2, seq_count)
    row, extra = lax.optimization_barrier((row, extra))
    row_prefix = prefix(row, pos_x)
    total = jnp.where(is_s, decay_of(chip) * row_prefix + chip, chip)
    for m in range(1, line):
        part = row[line - 1 - m]
        valid = pos_x <= line - 1 - m
        total = jnp.where(
            is_s, jnp.where(valid, decay_of(part) * total + part, total), total * decay_of(part)
        )
    col = gather_line(total, line, 2 * line, seq_count)
    col_prefix = prefix(col, pos_y)
    state = (decay_of(row_prefix) * col_prefix + row_prefix)[:, :HD]
    handed = lax.ppermute(
        decay[:, None, None] * state + mine, "seq", [(i, i ^ 1) for i in range(seq_count)]
    )
    return state, handed, extra


def local(query_vectors, key_vectors, value_vectors, decay_exp, norm_gain, out_weight, residual):
    tok_rows = query_vectors.shape[0]
    head_count = decay_exp.shape[0]
    query_heads = query_vectors.reshape(tok_rows, head_count, HD)
    key_heads = key_vectors.reshape(tok_rows, head_count, HD)
    value_heads = value_vectors.reshape(tok_rows, head_count, HD)
    local_exp = jnp.cumsum(decay_exp, axis=1)
    block_exp = local_exp[:, -1]
    local_rows = local_exp.T

    def local_attention(query_heads, key_heads, value_heads, local_exp):
        scores = jnp.einsum(
            "thd,shd->hts", query_heads, key_heads, preferred_element_type=jnp.float32
        )
        exp_gap = jnp.abs(local_exp[:, :, None] - local_exp[:, None, :])
        local_weights = (scores * factor(exp_gap)).astype(jnp.bfloat16)
        return jnp.einsum(
            "hts,shd->thd", local_weights, value_heads, preferred_element_type=jnp.float32
        )

    tail_factor = factor(block_exp[None, :] - local_rows)
    head_factor = factor(local_rows)
    second = (lax.axis_index("seq") % 2) == 1
    mine_factor = jnp.where(second, head_factor, tail_factor)
    other_factor = jnp.where(second, tail_factor, head_factor)
    keys_mine = (key_heads * mine_factor[:, :, None]).astype(jnp.bfloat16)
    keys_other = (key_heads * other_factor[:, :, None]).astype(jnp.bfloat16)
    summary_mine = jnp.einsum(
        "shd,she->hde", keys_mine, value_heads, preferred_element_type=jnp.float32
    )
    summary_other = jnp.einsum(
        "shd,she->hde", keys_other, value_heads, preferred_element_type=jnp.float32
    )
    block_decay = factor(block_exp)
    state_own, state_handed, local_part = block_scan(
        block_decay,
        summary_mine,
        summary_other,
        local_attention,
        (query_heads, key_heads, value_heads, local_exp),
    )
    remote_own = jnp.einsum(
        "thd,hde->the", query_heads, state_own.astype(jnp.bfloat16),
        preferred_element_type=jnp.float32,
    )
    remote_handed = jnp.einsum(
        "thd,hde->the", query_heads, state_handed.astype(jnp.bfloat16),
        preferred_element_type=jnp.float32,
    )
    remote_fwd = jnp.where(second, remote_handed, remote_own) * head_factor[:, :, None]
    remote_bwd = jnp.where(second, remote_own, remote_handed) * tail_factor[:, :, None]
    attention = local_part + remote_fwd + remote_bwd
    scale = lax.rsqrt(jnp.mean(attention * attention, axis=-1, keepdims=True) + 1e-06)
    normed = (attention * scale * norm_gain.reshape(head_count, HD)[None, :, :]).astype(
        jnp.bfloat16
    )
    normed = normed.reshape(tok_rows, head_count * HD)
    mixed = jnp.dot(
        lax.all_gather(normed, "tp", axis=1, tiled=True),
        out_weight,
        preferred_element_type=jnp.float32,
    )
    return (residual.astype(jnp.float32) + mixed).astype(jnp.bfloat16)


def solution(mesh):
    in_specs = (
        P("seq", "tp"),
        P("seq", "tp"),
        P("seq", "tp"),
        P("tp", "seq"),
        P("tp"),
        P(None, "tp"),
        P("seq", "tp"),
    )
    out_specs = P("seq", "tp")
    return jax.shard_map(local, mesh=mesh, in_specs=in_specs, out_specs=out_specs, check_vma=False)
```

```python
import jax
import jax.numpy as jnp
from jax import lax
from jax.sharding import PartitionSpec as P

HD = 128


def factor(exponents):
    return jnp.exp2(-exponents.astype(jnp.float32) / 16.0)


def pack(summary, decay):
    heads = decay.shape[0]
    return jnp.concatenate(
        [summary, jnp.broadcast_to(decay[:, None, None], (heads, 8, HD))], axis=1
    )


def gather_line(packed, line, stride, seq_count):
    got = []
    for shift in range(1, line):
        pairs = []
        for i in range(seq_count):
            at = (i // stride) % line
            step = -shift if i % 2 else shift
            pairs.append((i, i + (((at + step) % line) - at) * stride))
        got.append(lax.ppermute(packed, "seq", pairs))
    return got


def block_scan(decay, mine, other, extra):
    seq_count = lax.axis_size("seq")
    line = 4
    me = lax.axis_index("seq")
    second = (me % 2) == 1
    x = (me // 2) % line
    y = me // (2 * line)
    pos_x = jnp.where(second, line - 1 - x, x)
    pos_y = jnp.where(second, line - 1 - y, y)
    is_s = lax.broadcasted_iota(jnp.int32, (1, HD + 8, 1), 1) < HD

    def decay_of(packed):
        return packed[:, HD : HD + 1, 0:1]

    own = pack(mine, decay)
    got = lax.ppermute(pack(other, decay), "seq", [(i, i ^ 1) for i in range(seq_count)])
    chip = decay_of(got) * own + jnp.where(is_s, got, 0.0)

    def prefix(got, pos):
        acc = jnp.where(is_s, 0.0, 1.0) * jnp.ones_like(chip)
        for m, part in enumerate(got, start=1):
            acc = jnp.where(pos >= m, decay_of(acc) * part + jnp.where(is_s, acc, 0.0), acc)
        return acc

    row = gather_line(chip, line, 2, seq_count)
    row_prefix = prefix(row, pos_x)
    total = jnp.where(is_s, decay_of(chip) * row_prefix + chip, chip)
    for m in range(1, line):
        part = row[line - 1 - m]
        valid = pos_x <= line - 1 - m
        total = jnp.where(
            is_s, jnp.where(valid, decay_of(part) * total + part, total), total * decay_of(part)
        )
    col = gather_line(total, line, 2 * line, seq_count)
    col, extra = lax.optimization_barrier((col, extra))
    col_prefix = prefix(col, pos_y)
    state = (decay_of(row_prefix) * col_prefix + row_prefix)[:, :HD]
    handed = lax.ppermute(
        decay[:, None, None] * state + mine, "seq", [(i, i ^ 1) for i in range(seq_count)]
    )
    state_fwd = jnp.where(second, handed, state)
    state_bwd = jnp.where(second, state, handed)
    return state_fwd, state_bwd, extra


def local(query_vectors, key_vectors, value_vectors, decay_exp, norm_gain, out_weight, residual):
    tok_rows = query_vectors.shape[0]
    head_count = decay_exp.shape[0]
    query_heads = query_vectors.reshape(tok_rows, head_count, HD)
    key_heads = key_vectors.reshape(tok_rows, head_count, HD)
    value_heads = value_vectors.reshape(tok_rows, head_count, HD)
    local_exp = jnp.cumsum(decay_exp, axis=1)
    block_exp = local_exp[:, -1]
    local_rows = local_exp.T
    scores = jnp.einsum("thd,shd->hts", query_heads, key_heads, preferred_element_type=jnp.float32)
    exp_gap = jnp.abs(local_exp[:, :, None] - local_exp[:, None, :])
    local_weights = (scores * factor(exp_gap)).astype(jnp.bfloat16)
    local_part = jnp.einsum(
        "hts,shd->thd", local_weights, value_heads, preferred_element_type=jnp.float32
    )
    tail_factor = factor(block_exp[None, :] - local_rows)
    head_factor = factor(local_rows)
    second = (lax.axis_index("seq") % 2) == 1
    mine_factor = jnp.where(second, head_factor, tail_factor)
    other_factor = jnp.where(second, tail_factor, head_factor)
    keys_mine = (key_heads * mine_factor[:, :, None]).astype(jnp.bfloat16)
    keys_other = (key_heads * other_factor[:, :, None]).astype(jnp.bfloat16)
    summary_mine = jnp.einsum(
        "shd,she->hde", keys_mine, value_heads, preferred_element_type=jnp.float32
    )
    summary_other = jnp.einsum(
        "shd,she->hde", keys_other, value_heads, preferred_element_type=jnp.float32
    )
    block_decay = factor(block_exp)
    state_fwd, state_bwd, local_part = block_scan(
        block_decay, summary_mine, summary_other, local_part
    )
    state_fwd = state_fwd.astype(jnp.bfloat16)
    state_bwd = state_bwd.astype(jnp.bfloat16)
    remote_fwd = (
        jnp.einsum("thd,hde->the", query_heads, state_fwd, preferred_element_type=jnp.float32)
        * head_factor[:, :, None]
    )
    remote_bwd = (
        jnp.einsum("thd,hde->the", query_heads, state_bwd, preferred_element_type=jnp.float32)
        * tail_factor[:, :, None]
    )
    attention = local_part + remote_fwd + remote_bwd
    scale = lax.rsqrt(jnp.mean(attention * attention, axis=-1, keepdims=True) + 1e-06)
    normed = (attention * scale * norm_gain.reshape(head_count, HD)[None, :, :]).astype(
        jnp.bfloat16
    )
    normed = normed.reshape(tok_rows, head_count * HD)
    mixed = jnp.dot(
        lax.all_gather(normed, "tp", axis=1, tiled=True),
        out_weight,
        preferred_element_type=jnp.float32,
    )
    return (residual.astype(jnp.float32) + mixed).astype(jnp.bfloat16)


def solution(mesh):
    in_specs = (
        P("seq", "tp"),
        P("seq", "tp"),
        P("seq", "tp"),
        P("tp", "seq"),
        P("tp"),
        P(None, "tp"),
        P("seq", "tp"),
    )
    out_specs = P("seq", "tp")
    return jax.shard_map(local, mesh=mesh, in_specs=in_specs, out_specs=out_specs, check_vma=False)
```

```python
import jax
import jax.numpy as jnp
from jax import lax
from jax.sharding import PartitionSpec as P

HD = 128


def factor(exponents):
    return jnp.exp2(-exponents.astype(jnp.float32) / 16.0)


def pack(summary, decay):
    heads = decay.shape[0]
    return jnp.concatenate(
        [summary, jnp.broadcast_to(decay[:, None, None], (heads, 8, HD))], axis=1
    )


def gather_line(packed, line, stride, seq_count):
    got = []
    for shift in range(1, line):
        pairs = []
        for i in range(seq_count):
            at = (i // stride) % line
            step = -shift if i % 2 else shift
            pairs.append((i, i + (((at + step) % line) - at) * stride))
        got.append(lax.ppermute(packed, "seq", pairs))
    return got


def block_scan(decay, mine, other, extra, own_fn=None):
    seq_count = lax.axis_size("seq")
    line = 4
    me = lax.axis_index("seq")
    second = (me % 2) == 1
    x = (me // 2) % line
    y = me // (2 * line)
    pos_x = jnp.where(second, line - 1 - x, x)
    pos_y = jnp.where(second, line - 1 - y, y)
    is_s = lax.broadcasted_iota(jnp.int32, (1, HD + 8, 1), 1) < HD

    def decay_of(packed):
        return packed[:, HD : HD + 1, 0:1]

    own = pack(mine, decay)
    got = lax.ppermute(pack(other, decay), "seq", [(i, i ^ 1) for i in range(seq_count)])
    chip = decay_of(got) * own + jnp.where(is_s, got, 0.0)

    def prefix(got, pos):
        acc = jnp.where(is_s, 0.0, 1.0) * jnp.ones_like(chip)
        for m, part in enumerate(got, start=1):
            acc = jnp.where(pos >= m, decay_of(acc) * part + jnp.where(is_s, acc, 0.0), acc)
        return acc

    row = gather_line(chip, line, 2, seq_count)
    row_prefix = prefix(row, pos_x)
    total = jnp.where(is_s, decay_of(chip) * row_prefix + chip, chip)
    for m in range(1, line):
        part = row[line - 1 - m]
        valid = pos_x <= line - 1 - m
        total = jnp.where(
            is_s, jnp.where(valid, decay_of(part) * total + part, total), total * decay_of(part)
        )
    col = gather_line(total, line, 2 * line, seq_count)
    col, extra = lax.optimization_barrier((col, extra))
    col_prefix = prefix(col, pos_y)
    state = (decay_of(row_prefix) * col_prefix + row_prefix)[:, :HD]
    handed = lax.ppermute(
        decay[:, None, None] * state + mine, "seq", [(i, i ^ 1) for i in range(seq_count)]
    )
    if own_fn is None:
        return state, handed, extra
    handed, own = lax.optimization_barrier((handed, own_fn(state)))
    return own, handed, extra


def local(query_vectors, key_vectors, value_vectors, decay_exp, norm_gain, out_weight, residual):
    tok_rows = query_vectors.shape[0]
    head_count = decay_exp.shape[0]
    query_heads = query_vectors.reshape(tok_rows, head_count, HD)
    key_heads = key_vectors.reshape(tok_rows, head_count, HD)
    value_heads = value_vectors.reshape(tok_rows, head_count, HD)
    local_exp = jnp.cumsum(decay_exp, axis=1)
    block_exp = local_exp[:, -1]
    local_rows = local_exp.T
    scores = jnp.einsum("thd,shd->hts", query_heads, key_heads, preferred_element_type=jnp.float32)
    exp_gap = jnp.abs(local_exp[:, :, None] - local_exp[:, None, :])
    local_weights = (scores * factor(exp_gap)).astype(jnp.bfloat16)
    local_part = jnp.einsum(
        "hts,shd->thd", local_weights, value_heads, preferred_element_type=jnp.float32
    )
    tail_factor = factor(block_exp[None, :] - local_rows)
    head_factor = factor(local_rows)
    second = (lax.axis_index("seq") % 2) == 1
    mine_factor = jnp.where(second, head_factor, tail_factor)
    other_factor = jnp.where(second, tail_factor, head_factor)
    keys_mine = (key_heads * mine_factor[:, :, None]).astype(jnp.bfloat16)
    keys_other = (key_heads * other_factor[:, :, None]).astype(jnp.bfloat16)
    summary_mine = jnp.einsum(
        "shd,she->hde", keys_mine, value_heads, preferred_element_type=jnp.float32
    )
    summary_other = jnp.einsum(
        "shd,she->hde", keys_other, value_heads, preferred_element_type=jnp.float32
    )
    block_decay = factor(block_exp)
    def project(state):
        return jnp.einsum(
            "thd,hde->the",
            query_heads,
            state.astype(jnp.bfloat16),
            preferred_element_type=jnp.float32,
        )

    remote_own, state_handed, local_part = block_scan(
        block_decay, summary_mine, summary_other, local_part, project
    )
    remote_handed = project(state_handed)
    remote_fwd = jnp.where(second, remote_handed, remote_own) * head_factor[:, :, None]
    remote_bwd = jnp.where(second, remote_own, remote_handed) * tail_factor[:, :, None]
    attention = local_part + remote_fwd + remote_bwd
    scale = lax.rsqrt(jnp.mean(attention * attention, axis=-1, keepdims=True) + 1e-06)
    normed = (attention * scale * norm_gain.reshape(head_count, HD)[None, :, :]).astype(
        jnp.bfloat16
    )
    normed = normed.reshape(tok_rows, head_count * HD)
    mixed = jnp.dot(
        lax.all_gather(normed, "tp", axis=1, tiled=True),
        out_weight,
        preferred_element_type=jnp.float32,
    )
    return (residual.astype(jnp.float32) + mixed).astype(jnp.bfloat16)


def solution(mesh):
    in_specs = (
        P("seq", "tp"),
        P("seq", "tp"),
        P("seq", "tp"),
        P("tp", "seq"),
        P("tp"),
        P(None, "tp"),
        P("seq", "tp"),
    )
    out_specs = P("seq", "tp")
    return jax.shard_map(local, mesh=mesh, in_specs=in_specs, out_specs=out_specs, check_vma=False)
```

```python
import jax
import jax.numpy as jnp
from jax import lax
from jax.sharding import PartitionSpec as P

HD = 128


def factor(exponents):
    return jnp.exp2(-exponents.astype(jnp.float32) / 16.0)


def pack(summary, decay):
    heads = decay.shape[0]
    return jnp.concatenate(
        [summary, jnp.broadcast_to(decay[:, None, None], (heads, 8, HD))], axis=1
    )


def gather_line(packed, line, stride, seq_count):
    got = []
    for shift in range(1, line):
        pairs = []
        for i in range(seq_count):
            at = (i // stride) % line
            step = -shift if i % 2 else shift
            pairs.append((i, i + (((at + step) % line) - at) * stride))
        got.append(lax.ppermute(packed, "seq", pairs))
    return got


def block_scan(decay, mine, other, extra):
    seq_count = lax.axis_size("seq")
    line = 4
    me = lax.axis_index("seq")
    second = (me % 2) == 1
    x = (me // 2) % line
    y = me // (2 * line)
    pos_x = jnp.where(second, line - 1 - x, x)
    pos_y = jnp.where(second, line - 1 - y, y)
    is_s = lax.broadcasted_iota(jnp.int32, (1, HD + 8, 1), 1) < HD

    def decay_of(packed):
        return packed[:, HD : HD + 1, 0:1]

    own = pack(mine, decay)
    got = lax.ppermute(pack(other, decay), "seq", [(i, i ^ 1) for i in range(seq_count)])
    chip = decay_of(got) * own + jnp.where(is_s, got, 0.0)

    def prefix(got, pos):
        acc = jnp.where(is_s, 0.0, 1.0) * jnp.ones_like(chip)
        for m, part in enumerate(got, start=1):
            acc = jnp.where(pos >= m, decay_of(acc) * part + jnp.where(is_s, acc, 0.0), acc)
        return acc

    row = gather_line(chip, line, 2, seq_count)
    row_prefix = prefix(row, pos_x)
    total = jnp.where(is_s, decay_of(chip) * row_prefix + chip, chip)
    for m in range(1, line):
        part = row[line - 1 - m]
        valid = pos_x <= line - 1 - m
        total = jnp.where(
            is_s, jnp.where(valid, decay_of(part) * total + part, total), total * decay_of(part)
        )
    col = gather_line(total, line, 2 * line, seq_count)
    col, extra = lax.optimization_barrier((col, extra))
    col_prefix = prefix(col, pos_y)
    state = (decay_of(row_prefix) * col_prefix + row_prefix)[:, :HD]
    handed = lax.ppermute(
        decay[:, None, None] * state + mine, "seq", [(i, i ^ 1) for i in range(seq_count)]
    )
    state_fwd = jnp.where(second, handed, state)
    state_bwd = jnp.where(second, state, handed)
    return state_fwd, state_bwd, extra


def local(query_vectors, key_vectors, value_vectors, decay_exp, norm_gain, out_weight, residual):
    tok_rows = query_vectors.shape[0]
    head_count = decay_exp.shape[0]
    query_heads = query_vectors.reshape(tok_rows, head_count, HD)
    key_heads = key_vectors.reshape(tok_rows, head_count, HD)
    value_heads = value_vectors.reshape(tok_rows, head_count, HD)
    local_exp = jnp.cumsum(decay_exp, axis=1)
    block_exp = local_exp[:, -1]
    local_rows = local_exp.T
    scores = jnp.einsum("thd,shd->hts", query_heads, key_heads, preferred_element_type=jnp.float32)
    exp_gap = jnp.abs(local_exp[:, :, None] - local_exp[:, None, :])
    local_weights = (scores * factor(exp_gap)).astype(jnp.bfloat16)
    local_part = jnp.einsum(
        "hts,shd->thd", local_weights, value_heads, preferred_element_type=jnp.float32
    )
    tail_factor = factor(block_exp[None, :] - local_rows)
    head_factor = factor(local_rows)
    second = (lax.axis_index("seq") % 2) == 1
    mine_factor = jnp.where(second, head_factor, tail_factor)
    other_factor = jnp.where(second, tail_factor, head_factor)
    keys_mine = (key_heads * mine_factor[:, :, None]).astype(jnp.bfloat16)
    keys_other = (key_heads * other_factor[:, :, None]).astype(jnp.bfloat16)
    summary_mine = jnp.einsum(
        "shd,she->hde", keys_mine, value_heads, preferred_element_type=jnp.float32
    )
    summary_other = jnp.einsum(
        "shd,she->hde", keys_other, value_heads, preferred_element_type=jnp.float32
    )
    block_decay = factor(block_exp)
    state_fwd, state_bwd, local_part = block_scan(
        block_decay, summary_mine, summary_other, local_part
    )
    state_fwd = state_fwd.astype(jnp.bfloat16)
    state_bwd = state_bwd.astype(jnp.bfloat16)
    remote_fwd = (
        jnp.einsum("thd,hde->the", query_heads, state_fwd, preferred_element_type=jnp.float32)
        * head_factor[:, :, None]
    )
    remote_bwd = (
        jnp.einsum("thd,hde->the", query_heads, state_bwd, preferred_element_type=jnp.float32)
        * tail_factor[:, :, None]
    )
    attention = local_part + remote_fwd + remote_bwd
    scale = lax.rsqrt(jnp.mean(attention * attention, axis=-1, keepdims=True) + 1e-06)
    normed = (attention * scale * norm_gain.reshape(head_count, HD)[None, :, :]).astype(
        jnp.bfloat16
    )
    tp_count = lax.axis_size("tp")
    gathered = lax.all_gather(normed.transpose(1, 0, 2)[None], "tp", axis=0, tiled=True)
    mixed = lax.dot_general(
        gathered,
        out_weight.reshape(tp_count, head_count, HD, -1),
        (((0, 1, 3), (0, 1, 2)), ((), ())),
        preferred_element_type=jnp.float32,
    )
    return (residual.astype(jnp.float32) + mixed).astype(jnp.bfloat16)


def solution(mesh):
    in_specs = (
        P("seq", "tp"),
        P("seq", "tp"),
        P("seq", "tp"),
        P("tp", "seq"),
        P("tp"),
        P(None, "tp"),
        P("seq", "tp"),
    )
    out_specs = P("seq", "tp")
    return jax.shard_map(local, mesh=mesh, in_specs=in_specs, out_specs=out_specs, check_vma=False)
```

```python
import jax
import jax.numpy as jnp
from jax import lax
from jax.sharding import PartitionSpec as P

HD = 128


def factor(exponents):
    return jnp.exp2(-exponents.astype(jnp.float32) / 16.0)


def pack(summary, decay):
    heads = decay.shape[0]
    return jnp.concatenate(
        [summary, jnp.broadcast_to(decay[:, None, None], (heads, 8, HD))], axis=1
    )


def gather_line(packed, line, stride, seq_count):
    got = []
    for shift in range(1, line):
        pairs = []
        for i in range(seq_count):
            at = (i // stride) % line
            step = -shift if i % 2 else shift
            pairs.append((i, i + (((at + step) % line) - at) * stride))
        got.append(lax.ppermute(packed, "seq", pairs))
    return got


def block_scan(decay, mine, other, extra):
    seq_count = lax.axis_size("seq")
    line = 4
    me = lax.axis_index("seq")
    second = (me % 2) == 1
    x = (me // 2) % line
    y = me // (2 * line)
    pos_x = jnp.where(second, line - 1 - x, x)
    pos_y = jnp.where(second, line - 1 - y, y)
    is_s = lax.broadcasted_iota(jnp.int32, (1, HD + 8, 1), 1) < HD

    def decay_of(packed):
        return packed[:, HD : HD + 1, 0:1]

    own = pack(mine, decay)
    got = lax.ppermute(pack(other, decay), "seq", [(i, i ^ 1) for i in range(seq_count)])
    chip = decay_of(got) * own + jnp.where(is_s, got, 0.0)

    def prefix(got, pos):
        acc = jnp.where(is_s, 0.0, 1.0) * jnp.ones_like(chip)
        for m, part in enumerate(got, start=1):
            acc = jnp.where(pos >= m, decay_of(acc) * part + jnp.where(is_s, acc, 0.0), acc)
        return acc

    row = gather_line(chip, line, 2, seq_count)
    row_prefix = prefix(row, pos_x)
    total = jnp.where(is_s, decay_of(chip) * row_prefix + chip, chip)
    for m in range(1, line):
        part = row[line - 1 - m]
        valid = pos_x <= line - 1 - m
        total = jnp.where(
            is_s, jnp.where(valid, decay_of(part) * total + part, total), total * decay_of(part)
        )
    col = gather_line(total, line, 2 * line, seq_count)
    col, extra = lax.optimization_barrier((col, extra))
    col_prefix = prefix(col, pos_y)
    state = (decay_of(row_prefix) * col_prefix + row_prefix)[:, :HD]
    handed = lax.ppermute(
        decay[:, None, None] * state + mine, "seq", [(i, i ^ 1) for i in range(seq_count)]
    )
    state_fwd = jnp.where(second, handed, state)
    state_bwd = jnp.where(second, state, handed)
    return state_fwd, state_bwd, extra


def local(query_vectors, key_vectors, value_vectors, decay_exp, norm_gain, out_weight, residual):
    tok_rows = query_vectors.shape[0]
    head_count = decay_exp.shape[0]
    query_heads = query_vectors.reshape(tok_rows, head_count, HD)
    key_heads = key_vectors.reshape(tok_rows, head_count, HD)
    value_heads = value_vectors.reshape(tok_rows, head_count, HD)
    tok_dev = decay_exp.shape[1]
    upper = (
        lax.broadcasted_iota(jnp.int32, (tok_dev, tok_dev), 0)
        <= lax.broadcasted_iota(jnp.int32, (tok_dev, tok_dev), 1)
    ).astype(jnp.float32)
    local_exp = jnp.dot(
        decay_exp.astype(jnp.float32), upper, precision=lax.Precision.HIGHEST,
        preferred_element_type=jnp.float32,
    ).astype(jnp.int32)
    block_exp = local_exp[:, -1]
    local_rows = local_exp.T
    scores = jnp.einsum("thd,shd->hts", query_heads, key_heads, preferred_element_type=jnp.float32)
    exp_gap = jnp.abs(local_exp[:, :, None] - local_exp[:, None, :])
    local_weights = (scores * factor(exp_gap)).astype(jnp.bfloat16)
    local_part = jnp.einsum(
        "hts,shd->thd", local_weights, value_heads, preferred_element_type=jnp.float32
    )
    tail_factor = factor(block_exp[None, :] - local_rows)
    head_factor = factor(local_rows)
    second = (lax.axis_index("seq") % 2) == 1
    mine_factor = jnp.where(second, head_factor, tail_factor)
    other_factor = jnp.where(second, tail_factor, head_factor)
    keys_mine = (key_heads * mine_factor[:, :, None]).astype(jnp.bfloat16)
    keys_other = (key_heads * other_factor[:, :, None]).astype(jnp.bfloat16)
    summary_mine = jnp.einsum(
        "shd,she->hde", keys_mine, value_heads, preferred_element_type=jnp.float32
    )
    summary_other = jnp.einsum(
        "shd,she->hde", keys_other, value_heads, preferred_element_type=jnp.float32
    )
    block_decay = factor(block_exp)
    state_fwd, state_bwd, local_part = block_scan(
        block_decay, summary_mine, summary_other, local_part
    )
    state_fwd = state_fwd.astype(jnp.bfloat16)
    state_bwd = state_bwd.astype(jnp.bfloat16)
    remote_fwd = (
        jnp.einsum("thd,hde->the", query_heads, state_fwd, preferred_element_type=jnp.float32)
        * head_factor[:, :, None]
    )
    remote_bwd = (
        jnp.einsum("thd,hde->the", query_heads, state_bwd, preferred_element_type=jnp.float32)
        * tail_factor[:, :, None]
    )
    attention = local_part + remote_fwd + remote_bwd
    scale = lax.rsqrt(jnp.mean(attention * attention, axis=-1, keepdims=True) + 1e-06)
    normed = (attention * scale * norm_gain.reshape(head_count, HD)[None, :, :]).astype(
        jnp.bfloat16
    )
    tp_count = lax.axis_size("tp")
    gathered = lax.all_gather(normed.transpose(1, 0, 2)[None], "tp", axis=0, tiled=True)
    mixed = lax.dot_general(
        gathered,
        out_weight.reshape(tp_count, head_count, HD, -1),
        (((0, 1, 3), (0, 1, 2)), ((), ())),
        preferred_element_type=jnp.float32,
    )
    return (residual.astype(jnp.float32) + mixed).astype(jnp.bfloat16)


def solution(mesh):
    in_specs = (
        P("seq", "tp"),
        P("seq", "tp"),
        P("seq", "tp"),
        P("tp", "seq"),
        P("tp"),
        P(None, "tp"),
        P("seq", "tp"),
    )
    out_specs = P("seq", "tp")
    return jax.shard_map(local, mesh=mesh, in_specs=in_specs, out_specs=out_specs, check_vma=False)
```

```python
import jax
import jax.numpy as jnp
from jax import lax
from jax.sharding import PartitionSpec as P

HD = 128


def factor(exponents):
    return jnp.exp2(-exponents.astype(jnp.float32) / 16.0)


def pack(summary, decay):
    heads = decay.shape[0]
    return jnp.concatenate(
        [summary, jnp.broadcast_to(decay[:, None, None], (heads, 8, HD))], axis=1
    )


def gather_line(packed, line, stride, seq_count):
    got = []
    for shift in range(1, line):
        pairs = []
        for i in range(seq_count):
            at = (i // stride) % line
            step = -shift if i % 2 else shift
            pairs.append((i, i + (((at + step) % line) - at) * stride))
        sent = lax.ppermute(packed.astype(jnp.bfloat16), "seq", pairs)
        got.append(sent.astype(jnp.float32))
    return got


def block_scan(decay, mine, other, extra):
    seq_count = lax.axis_size("seq")
    line = 4
    me = lax.axis_index("seq")
    second = (me % 2) == 1
    x = (me // 2) % line
    y = me // (2 * line)
    pos_x = jnp.where(second, line - 1 - x, x)
    pos_y = jnp.where(second, line - 1 - y, y)
    is_s = lax.broadcasted_iota(jnp.int32, (1, HD + 8, 1), 1) < HD

    def decay_of(packed):
        return packed[:, HD : HD + 1, 0:1]

    own = pack(mine, decay)
    got = lax.ppermute(pack(other, decay), "seq", [(i, i ^ 1) for i in range(seq_count)])
    chip = decay_of(got) * own + jnp.where(is_s, got, 0.0)

    def prefix(got, pos):
        acc = jnp.where(is_s, 0.0, 1.0) * jnp.ones_like(chip)
        for m, part in enumerate(got, start=1):
            acc = jnp.where(pos >= m, decay_of(acc) * part + jnp.where(is_s, acc, 0.0), acc)
        return acc

    row = gather_line(chip, line, 2, seq_count)
    row_prefix = prefix(row, pos_x)
    total = jnp.where(is_s, decay_of(chip) * row_prefix + chip, chip)
    for m in range(1, line):
        part = row[line - 1 - m]
        valid = pos_x <= line - 1 - m
        total = jnp.where(
            is_s, jnp.where(valid, decay_of(part) * total + part, total), total * decay_of(part)
        )
    col = gather_line(total, line, 2 * line, seq_count)
    col, extra = lax.optimization_barrier((col, extra))
    col_prefix = prefix(col, pos_y)
    state = (decay_of(row_prefix) * col_prefix + row_prefix)[:, :HD]
    handed = lax.ppermute(
        decay[:, None, None] * state + mine, "seq", [(i, i ^ 1) for i in range(seq_count)]
    )
    state_fwd = jnp.where(second, handed, state)
    state_bwd = jnp.where(second, state, handed)
    return state_fwd, state_bwd, extra


def local(query_vectors, key_vectors, value_vectors, decay_exp, norm_gain, out_weight, residual):
    tok_rows = query_vectors.shape[0]
    head_count = decay_exp.shape[0]
    query_heads = query_vectors.reshape(tok_rows, head_count, HD)
    key_heads = key_vectors.reshape(tok_rows, head_count, HD)
    value_heads = value_vectors.reshape(tok_rows, head_count, HD)
    tok_dev = decay_exp.shape[1]
    upper = (
        lax.broadcasted_iota(jnp.int32, (tok_dev, tok_dev), 0)
        <= lax.broadcasted_iota(jnp.int32, (tok_dev, tok_dev), 1)
    ).astype(jnp.float32)
    local_exp = jnp.dot(
        decay_exp.astype(jnp.float32), upper, precision=lax.Precision.HIGHEST,
        preferred_element_type=jnp.float32,
    ).astype(jnp.int32)
    block_exp = local_exp[:, -1]
    local_rows = local_exp.T
    scores = jnp.einsum("thd,shd->hts", query_heads, key_heads, preferred_element_type=jnp.float32)
    exp_gap = jnp.abs(local_exp[:, :, None] - local_exp[:, None, :])
    local_weights = (scores * factor(exp_gap)).astype(jnp.bfloat16)
    local_part = jnp.einsum(
        "hts,shd->thd", local_weights, value_heads, preferred_element_type=jnp.float32
    )
    tail_factor = factor(block_exp[None, :] - local_rows)
    head_factor = factor(local_rows)
    second = (lax.axis_index("seq") % 2) == 1
    mine_factor = jnp.where(second, head_factor, tail_factor)
    other_factor = jnp.where(second, tail_factor, head_factor)
    keys_mine = (key_heads * mine_factor[:, :, None]).astype(jnp.bfloat16)
    keys_other = (key_heads * other_factor[:, :, None]).astype(jnp.bfloat16)
    summary_mine = jnp.einsum(
        "shd,she->hde", keys_mine, value_heads, preferred_element_type=jnp.float32
    )
    summary_other = jnp.einsum(
        "shd,she->hde", keys_other, value_heads, preferred_element_type=jnp.float32
    )
    block_decay = factor(block_exp)
    state_fwd, state_bwd, local_part = block_scan(
        block_decay, summary_mine, summary_other, local_part
    )
    state_fwd = state_fwd.astype(jnp.bfloat16)
    state_bwd = state_bwd.astype(jnp.bfloat16)
    remote_fwd = (
        jnp.einsum("thd,hde->the", query_heads, state_fwd, preferred_element_type=jnp.float32)
        * head_factor[:, :, None]
    )
    remote_bwd = (
        jnp.einsum("thd,hde->the", query_heads, state_bwd, preferred_element_type=jnp.float32)
        * tail_factor[:, :, None]
    )
    attention = local_part + remote_fwd + remote_bwd
    scale = lax.rsqrt(jnp.mean(attention * attention, axis=-1, keepdims=True) + 1e-06)
    normed = (attention * scale * norm_gain.reshape(head_count, HD)[None, :, :]).astype(
        jnp.bfloat16
    )
    tp_count = lax.axis_size("tp")
    gathered = lax.all_gather(normed.transpose(1, 0, 2)[None], "tp", axis=0, tiled=True)
    mixed = lax.dot_general(
        gathered,
        out_weight.reshape(tp_count, head_count, HD, -1),
        (((0, 1, 3), (0, 1, 2)), ((), ())),
        preferred_element_type=jnp.float32,
    )
    return (residual.astype(jnp.float32) + mixed).astype(jnp.bfloat16)


def solution(mesh):
    in_specs = (
        P("seq", "tp"),
        P("seq", "tp"),
        P("seq", "tp"),
        P("tp", "seq"),
        P("tp"),
        P(None, "tp"),
        P("seq", "tp"),
    )
    out_specs = P("seq", "tp")
    return jax.shard_map(local, mesh=mesh, in_specs=in_specs, out_specs=out_specs, check_vma=False)
```

```python
import jax
import jax.numpy as jnp
from jax import lax
from jax.sharding import PartitionSpec as P

HD = 128


def factor(exponents):
    return jnp.exp2(-exponents.astype(jnp.float32) / 16.0)


def pack(summary, decay):
    heads = decay.shape[0]
    return jnp.concatenate(
        [summary, jnp.broadcast_to(decay[:, None, None], (heads, 8, HD))], axis=1
    )


def gather_line(packed, line, stride, seq_count, wrap=True):
    got = []
    for shift in range(1, line):
        pairs = []
        for i in range(seq_count):
            at = (i // stride) % line
            step = -shift if i % 2 else shift
            if wrap or 0 <= at + step < line:
                pairs.append((i, i + (((at + step) % line) - at) * stride))
        got.append(lax.ppermute(packed, "seq", pairs))
    return got


def block_scan(decay, mine, other, extra):
    seq_count = lax.axis_size("seq")
    line = 4
    me = lax.axis_index("seq")
    second = (me % 2) == 1
    x = (me // 2) % line
    y = me // (2 * line)
    pos_x = jnp.where(second, line - 1 - x, x)
    pos_y = jnp.where(second, line - 1 - y, y)
    is_s = lax.broadcasted_iota(jnp.int32, (1, HD + 8, 1), 1) < HD

    def decay_of(packed):
        return packed[:, HD : HD + 1, 0:1]

    own = pack(mine, decay)
    got = lax.ppermute(pack(other, decay), "seq", [(i, i ^ 1) for i in range(seq_count)])
    chip = decay_of(got) * own + jnp.where(is_s, got, 0.0)

    def prefix(got, pos):
        acc = jnp.where(is_s, 0.0, 1.0) * jnp.ones_like(chip)
        for m, part in enumerate(got, start=1):
            acc = jnp.where(pos >= m, decay_of(acc) * part + jnp.where(is_s, acc, 0.0), acc)
        return acc

    row = gather_line(chip, line, 2, seq_count)
    row_prefix = prefix(row, pos_x)
    total = jnp.where(is_s, decay_of(chip) * row_prefix + chip, chip)
    for m in range(1, line):
        part = row[line - 1 - m]
        valid = pos_x <= line - 1 - m
        total = jnp.where(
            is_s, jnp.where(valid, decay_of(part) * total + part, total), total * decay_of(part)
        )
    col = gather_line(total, line, 2 * line, seq_count, wrap=False)
    col, extra = lax.optimization_barrier((col, extra))
    col_prefix = prefix(col, pos_y)
    state = (decay_of(row_prefix) * col_prefix + row_prefix)[:, :HD]
    handed = lax.ppermute(
        decay[:, None, None] * state + mine, "seq", [(i, i ^ 1) for i in range(seq_count)]
    )
    state_fwd = jnp.where(second, handed, state)
    state_bwd = jnp.where(second, state, handed)
    return state_fwd, state_bwd, extra


def local(query_vectors, key_vectors, value_vectors, decay_exp, norm_gain, out_weight, residual):
    tok_rows = query_vectors.shape[0]
    head_count = decay_exp.shape[0]
    query_heads = query_vectors.reshape(tok_rows, head_count, HD)
    key_heads = key_vectors.reshape(tok_rows, head_count, HD)
    value_heads = value_vectors.reshape(tok_rows, head_count, HD)
    tok_dev = decay_exp.shape[1]
    upper = (
        lax.broadcasted_iota(jnp.int32, (tok_dev, tok_dev), 0)
        <= lax.broadcasted_iota(jnp.int32, (tok_dev, tok_dev), 1)
    ).astype(jnp.float32)
    local_exp = jnp.dot(
        decay_exp.astype(jnp.float32), upper, precision=lax.Precision.HIGHEST,
        preferred_element_type=jnp.float32,
    ).astype(jnp.int32)
    block_exp = local_exp[:, -1]
    local_rows = local_exp.T
    scores = jnp.einsum("thd,shd->hts", query_heads, key_heads, preferred_element_type=jnp.float32)
    exp_gap = jnp.abs(local_exp[:, :, None] - local_exp[:, None, :])
    local_weights = (scores * factor(exp_gap)).astype(jnp.bfloat16)
    local_part = jnp.einsum(
        "hts,shd->thd", local_weights, value_heads, preferred_element_type=jnp.float32
    )
    tail_factor = factor(block_exp[None, :] - local_rows)
    head_factor = factor(local_rows)
    second = (lax.axis_index("seq") % 2) == 1
    mine_factor = jnp.where(second, head_factor, tail_factor)
    other_factor = jnp.where(second, tail_factor, head_factor)
    keys_mine = (key_heads * mine_factor[:, :, None]).astype(jnp.bfloat16)
    keys_other = (key_heads * other_factor[:, :, None]).astype(jnp.bfloat16)
    summary_mine = jnp.einsum(
        "shd,she->hde", keys_mine, value_heads, preferred_element_type=jnp.float32
    )
    summary_other = jnp.einsum(
        "shd,she->hde", keys_other, value_heads, preferred_element_type=jnp.float32
    )
    block_decay = factor(block_exp)
    state_fwd, state_bwd, local_part = block_scan(
        block_decay, summary_mine, summary_other, local_part
    )
    state_fwd = state_fwd.astype(jnp.bfloat16)
    state_bwd = state_bwd.astype(jnp.bfloat16)
    remote_fwd = (
        jnp.einsum("thd,hde->the", query_heads, state_fwd, preferred_element_type=jnp.float32)
        * head_factor[:, :, None]
    )
    remote_bwd = (
        jnp.einsum("thd,hde->the", query_heads, state_bwd, preferred_element_type=jnp.float32)
        * tail_factor[:, :, None]
    )
    attention = local_part + remote_fwd + remote_bwd
    scale = lax.rsqrt(jnp.mean(attention * attention, axis=-1, keepdims=True) + 1e-06)
    normed = (attention * scale * norm_gain.reshape(head_count, HD)[None, :, :]).astype(
        jnp.bfloat16
    )
    tp_count = lax.axis_size("tp")
    gathered = lax.all_gather(normed.transpose(1, 0, 2)[None], "tp", axis=0, tiled=True)
    mixed = lax.dot_general(
        gathered,
        out_weight.reshape(tp_count, head_count, HD, -1),
        (((0, 1, 3), (0, 1, 2)), ((), ())),
        preferred_element_type=jnp.float32,
    )
    return (residual.astype(jnp.float32) + mixed).astype(jnp.bfloat16)


def solution(mesh):
    in_specs = (
        P("seq", "tp"),
        P("seq", "tp"),
        P("seq", "tp"),
        P("tp", "seq"),
        P("tp"),
        P(None, "tp"),
        P("seq", "tp"),
    )
    out_specs = P("seq", "tp")
    return jax.shard_map(local, mesh=mesh, in_specs=in_specs, out_specs=out_specs, check_vma=False)
```
